512 devices in a mesh: ctx: 128 (over y, z, core), tp: 4 (over x).
Axes of the slice: x: 4, y: 8, z: 8, core: 2. Of those that a mesh axis runs over, the one named last changes fastest.
Arguments:
- outer_gate: bfloat16 [32768, 2048], P('ctx', 'tp'), may hold values from -6 to 6
- inner_gate: bfloat16 [32768, 2048], P('ctx', 'tp'), may hold values from -6 to 6
- stream: bfloat16 [32768, 2048], P('ctx', 'tp'), may hold values from -6 to 6
- filters: bfloat16 [128, 128], P('tp'), may hold values from -1 to 1
- query_rows: bfloat16 [32768, 2048], P('ctx', 'tp'), may hold values from -49 to 49
- key_rows: bfloat16 [32768, 2048], P('ctx', 'tp'), may hold values from -4 to 4
Outputs:
- mixed: bfloat16 [32768, 2048], P('ctx', 'tp')
- attended: bfloat16 [32768, 2048], P('ctx', 'tp')
The draws below stay inside these ranges and needn't reach their ends.
All inputs are finite; a program needn't handle non-finite values.
Results may differ from the reference program's by a relative error of at most 0.007.
Values may be sent and summed in bfloat16 or wider, within the bound.
No kernel may reach another device: no remote copies, remote signals or barrier semaphores. Data moves between devices by JAX's collectives and lax.ppermute only.
A program may use at most 64 MiB of HBM per device.

```python
import math
import jax
import jax.numpy as jnp
from jax import lax

HEADS = 16
HEAD_DIM = 128
WIDTH = 2048
GROUP = 16
FILTER_GROUPS = 128
FILTER_TAPS = 128
LENGTH = 8192
TOKENS = 32768


def draw_filters(key, part):
    root_random_key = jax.random.fold_in(key, 11)
    decay_rate_key, jitter_random_key, spike_random_key = jax.random.split(root_random_key, 3)
    filter_tap_index = jnp.arange(FILTER_TAPS, dtype=jnp.float32)
    decay_length = FILTER_TAPS * jnp.exp(jax.random.uniform(decay_rate_key, (FILTER_GROUPS, 1), jnp.float32, math.log(0.15), math.log(8.0)))
    random_jitter = jax.random.truncated_normal(jitter_random_key, -4.0, 4.0, (FILTER_GROUPS, FILTER_TAPS), jnp.float32)
    spike_taps = jax.random.randint(spike_random_key, (FILTER_GROUPS, 3), 1, FILTER_TAPS)
    spike_count = jnp.sum((jnp.arange(FILTER_TAPS, dtype=jnp.int32)[None, None, :] >= spike_taps[:, :, None]).astype(jnp.float32), axis=1)
    return (0.25 * random_jitter * jnp.exp(-filter_tap_index[None, :] / decay_length) * jnp.exp(spike_count * math.log(0.6))).astype(jnp.bfloat16)


def draw_pair(key):
    root_random_key = jax.random.fold_in(key, 7)
    query_key, second_key = jax.random.split(root_random_key)
    queries = 2.0 * jax.random.truncated_normal(query_key, -5.0, 5.0, (TOKENS, WIDTH), jnp.float32)
    keys_drawn = jax.random.truncated_normal(second_key, -4.0, 4.0, (TOKENS, WIDTH), jnp.float32)
    return (queries, keys_drawn)


def draw_query_rows(key, part):
    return draw_pair(key)[0].astype(jnp.bfloat16)


def draw_key_rows(key, part):
    return draw_pair(key)[1].astype(jnp.bfloat16)


def steps_of(rng, dims, pieces, low, largest):
    level, own = 1.0, jax.random.fold_in(rng, 6)
    for axis_at, blocks in pieces:
        draws = jnp.exp(jax.random.uniform(jax.random.fold_in(own, axis_at), (blocks,), jnp.float32, low / len(pieces), largest / len(pieces)))
        level = level * jnp.repeat(draws, dims[axis_at] // blocks).reshape([-1 if axis == axis_at else 1 for axis in range(len(dims))])
    return level


def scatter_about(key, shape, width, reach, cuts=(), kind=jnp.bfloat16):
    values = jax.random.normal(key, shape, jnp.float32) * width
    if len(cuts) > 0:
        values = steps_of(key, shape, cuts, -0.22, 0.18) * values
    return jnp.clip(values, min=-reach, max=reach).astype(kind)


def setup_inputs(seed: int = 0) -> dict:
    keys = jax.random.split(jax.random.key(seed), 7)
    return {
        "outer_gate": scatter_about(keys[0], (TOKENS, WIDTH), 1.0, 6.0, ((0, 128), (1, 4))),
        "inner_gate": scatter_about(keys[1], (TOKENS, WIDTH), 1.0, 6.0, ((0, 128), (1, 4))),
        "stream": scatter_about(keys[2], (TOKENS, WIDTH), 1.0, 6.0, ((0, 128), (1, 4))),
        "filters": draw_filters(jax.random.fold_in(keys[6], 71), 0),
        "query_rows": draw_query_rows(jax.random.fold_in(keys[6], 71), 0),
        "key_rows": draw_key_rows(jax.random.fold_in(keys[6], 71), 0),
    }


def toeplitz_taps(filters, offset):
    tap_table = filters.astype(jnp.float32)
    tap_lags = jnp.arange(FILTER_TAPS, dtype=jnp.int32)[:, None] - jnp.arange(FILTER_TAPS, dtype=jnp.int32)[None, :] + offset
    in_range = (tap_lags >= 0) & (tap_lags < FILTER_TAPS)
    picked = jnp.take(tap_table, jnp.clip(tap_lags, 0, FILTER_TAPS - 1), axis=1)
    return jnp.where(in_range[None], picked, jnp.zeros_like(picked))

def reference(outer_gate, inner_gate, stream, filters, query_rows, key_rows):
    half_length = LENGTH // 2
    seq_count = TOKENS // LENGTH + 1

    def padded(array):
        return jnp.pad(array, ((half_length, half_length), (0, 0)))
    product = (inner_gate.astype(jnp.float32) * stream.astype(jnp.float32)).astype(jnp.bfloat16)
    blocks = padded(product).astype(jnp.float32).reshape(seq_count, LENGTH // FILTER_TAPS, FILTER_TAPS, FILTER_GROUPS, GROUP)
    before = jnp.pad(blocks, ((0, 0), (1, 0), (0, 0), (0, 0), (0, 0)))[:, :-1]
    near_taps = toeplitz_taps(filters, 0)
    far_taps = toeplitz_taps(filters, FILTER_TAPS)
    filtered = jnp.einsum('gts,absgc->abtgc', near_taps, blocks, precision=lax.Precision.HIGHEST)
    filtered = filtered + jnp.einsum('gts,absgc->abtgc', far_taps, before, precision=lax.Precision.HIGHEST)
    filtered = filtered.reshape(seq_count * LENGTH, WIDTH)
    mixed_long = (padded(outer_gate).astype(jnp.float32) * filtered).astype(jnp.bfloat16)
    query_block = min(512, LENGTH)
    score_scale = 1.0 / math.sqrt(HEAD_DIM)

    def by_head(array):
        return array.reshape(seq_count, LENGTH, HEADS, HEAD_DIM).transpose(0, 2, 1, 3).reshape(seq_count * HEADS, LENGTH, HEAD_DIM)
    key_pos = jnp.arange(LENGTH, dtype=jnp.int32)
    seq_ids = jnp.repeat(jnp.arange(seq_count, dtype=jnp.int32), HEADS)

    def one_pair(operands):
        queries, key_head, value_head, seq_id = operands
        key_real = seq_id * LENGTH + key_pos >= half_length

        def one_block(key_start):
            query_slab = lax.dynamic_slice_in_dim(queries, key_start, query_block, 0)
            scores = jnp.dot(query_slab, key_head.T, preferred_element_type=jnp.float32) * score_scale
            query_pos = key_start + jnp.arange(query_block, dtype=jnp.int32)
            allowed = (key_pos[None, :] <= query_pos[:, None]) & key_real[None, :]
            scores = jnp.where(allowed, scores, -1e+30)
            row_peak = lax.optimization_barrier(jnp.max(scores, axis=1, keepdims=True))
            exp_terms = jnp.where(allowed, jnp.exp(scores - row_peak), 0.0)
            row_total = jnp.maximum(lax.optimization_barrier(jnp.sum(exp_terms, axis=1, keepdims=True)), 1e-30)
            weights = exp_terms.astype(jnp.bfloat16)
            result = jnp.dot(weights, value_head, preferred_element_type=jnp.float32) / row_total
            return result.astype(jnp.bfloat16)
        starts = (jnp.arange(LENGTH // query_block, dtype=jnp.int32) * query_block).astype(jnp.int32)
        return lax.map(one_block, starts)
    results = lax.map(one_pair, (by_head(padded(query_rows)), by_head(padded(key_rows)), by_head(mixed_long), seq_ids))
    attended = results.reshape(seq_count, HEADS, LENGTH, HEAD_DIM).transpose(0, 2, 1, 3).reshape(seq_count * LENGTH, WIDTH)
    return (mixed_long[half_length:half_length + TOKENS], attended[half_length:half_length + TOKENS])
```

```python
import math

import jax
import jax.numpy as jnp
from jax import lax
from jax.sharding import PartitionSpec as P

HEAD_DIM = 128


NEGATIVE = -1e30


def passed_along(block, axis, distance):
    devices = range(lax.axis_size(axis))
    route = [(i - distance, i) for i in devices if i - distance in devices]
    return lax.ppermute(block, axis, route)


def toeplitz_taps(filters, offset):
    groups, kernel = filters.shape
    flipped = filters[:, ::-1]
    zeros = jnp.zeros_like(flipped)
    pieces = [flipped, zeros] if offset == 0 else [zeros, flipped]
    lags = jnp.concatenate(pieces, axis=1)
    flat = jnp.tile(lags, (1, kernel))[:, : kernel * (2 * kernel - 1)]
    return flat.reshape(groups, kernel, 2 * kernel - 1)[:, :, kernel - 1 : 2 * kernel - 1]


def apply_blocks(matrix, blocks):
    return jnp.einsum("gts,bsgc->btgc", matrix, blocks, preferred_element_type=jnp.float32)


def body(outer_gate, inner_gate, stream, filters, query_rows, key_rows):
    row_count, channels = outer_gate.shape
    groups, kernel = filters.shape
    group_size = channels // groups
    seq_span = min(8192 // row_count, lax.axis_size("ctx") // 2)
    half_span = seq_span // 2
    shard_index = lax.axis_index("ctx")
    seq_place = (shard_index + half_span) % seq_span
    product = (inner_gate.astype(jnp.float32) * stream.astype(jnp.float32)).astype(jnp.bfloat16)
    blocks = product.reshape(row_count // kernel, kernel, groups, group_size)
    near_taps = toeplitz_taps(filters, 0)
    far_taps = toeplitz_taps(filters, kernel)
    tail_rows = product[row_count - kernel + 1 :]
    earlier = passed_along(tail_rows, "ctx", 1)
    earlier = jnp.where(seq_place == 0, jnp.zeros_like(earlier), earlier)
    first_block = jnp.concatenate([jnp.zeros((1, channels), jnp.bfloat16), earlier], 0)
    first_block = first_block.reshape(1, kernel, groups, group_size)
    before = jnp.concatenate([first_block, blocks[:-1]], 0)
    filtered = (apply_blocks(near_taps, blocks) + apply_blocks(far_taps, before)).reshape(
        row_count, channels
    )
    mixed = (outer_gate.astype(jnp.float32) * filtered).astype(jnp.bfloat16)
    local_heads = channels // HEAD_DIM
    queries = query_rows.reshape(row_count, local_heads, HEAD_DIM)
    score_scale = 1.0 / math.sqrt(HEAD_DIM)
    query_pos = shard_index * row_count + jnp.arange(row_count, dtype=jnp.int32)
    seq_start = jnp.maximum(shard_index - seq_place, 0) * row_count
    win_shards = 2
    win_shards = min(win_shards, seq_span)
    kv_rows = jnp.stack([key_rows, mixed])
    reached = 1
    while reached < win_shards:
        arrived = passed_along(kv_rows, "ctx", reached)
        kv_rows = jnp.concatenate([arrived, kv_rows], 1)
        reached = reached * 2

    def attend(attn_state, window, first_shard):
        window_rows = window.shape[1]
        step_rows = min(512, window_rows)
        block_count = window_rows // step_rows
        split_window = window.reshape(2, block_count, step_rows, local_heads, HEAD_DIM)
        starts = first_shard * row_count + jnp.arange(block_count, dtype=jnp.int32) * step_rows

        def one_block(carried, block_item):
            key_block, value_block, key_start = block_item
            weighted, row_peak, row_total = carried
            scores = (
                jnp.einsum("qhd,khd->hqk", queries, key_block, preferred_element_type=jnp.float32)
                * score_scale
            )
            key_pos = key_start + jnp.arange(step_rows, dtype=jnp.int32)
            visible_keys = (key_pos[None, :] >= seq_start) & (
                key_pos[None, :] <= query_pos[:, None]
            )
            scores = jnp.where(visible_keys[None], scores, NEGATIVE)
            new_peak = jnp.maximum(row_peak, jnp.max(scores, axis=2))
            exp_terms = jnp.where(visible_keys[None], jnp.exp(scores - new_peak[..., None]), 0.0)
            rescale = jnp.exp(row_peak - new_peak)
            row_total = row_total * rescale + jnp.sum(exp_terms, axis=2)
            weights = exp_terms.astype(jnp.bfloat16)
            weighted = weighted * rescale[..., None] + jnp.einsum(
                "hqk,khd->hqd", weights, value_block, preferred_element_type=jnp.float32
            )
            return ((weighted, new_peak, row_total), None)

        attn_state, unused = lax.scan(
            one_block, attn_state, (split_window[0], split_window[1], starts)
        )
        return attn_state

    def visit(attn_state, window, first_shard):
        return attend(attn_state, window, first_shard)

    attn_state = (
        jnp.zeros((local_heads, row_count, HEAD_DIM), jnp.float32),
        jnp.full((local_heads, row_count), NEGATIVE, jnp.float32),
        jnp.zeros((local_heads, row_count), jnp.float32),
    )
    attn_state = visit(attn_state, kv_rows, shard_index - (win_shards - 1))

    def relay(turn_index, carried):
        window, held_state = carried
        window = passed_along(window, "ctx", win_shards)
        first_shard = shard_index - win_shards * (turn_index + 1) - (win_shards - 1)
        return (window, visit(held_state, window, first_shard))

    kv_rows, attn_state = lax.fori_loop(0, seq_span // win_shards - 1, relay, (kv_rows, attn_state))
    weighted, row_peak, row_total = attn_state
    attended = (
        (weighted / row_total[..., None])
        .transpose(1, 0, 2)
        .reshape(row_count, channels)
        .astype(jnp.bfloat16)
    )
    return (mixed, attended)


def solution(mesh):
    in_specs = (
        P("ctx", "tp"),
        P("ctx", "tp"),
        P("ctx", "tp"),
        P("tp", None),
        P("ctx", "tp"),
        P("ctx", "tp"),
    )
    out_specs = (P("ctx", "tp"), P("ctx", "tp"))
    return jax.shard_map(body, mesh=mesh, in_specs=in_specs, out_specs=out_specs, check_vma=False)
```

```python
import functools
import math

import jax
import jax.numpy as jnp
from jax import lax
from jax.sharding import Mesh, NamedSharding
from jax.sharding import PartitionSpec as P

HEAD_DIM = 128
LENGTH = 8192
CORES = 2
WINDOW_SHARDS = 8

NEGATIVE = -1e30
CTX_AXES = ("row", "col", "core")


def passed_along(block, axis, size, distance):
    route = [(i - distance, i) for i in range(size) if i - distance >= 0]
    return lax.ppermute(block, axis, route)


def toeplitz_taps(filters, offset):
    groups, kernel = filters.shape
    flipped = filters[:, ::-1]
    zeros = jnp.zeros_like(flipped)
    pieces = [flipped, zeros] if offset == 0 else [zeros, flipped]
    lags = jnp.concatenate(pieces, axis=1)
    flat = jnp.tile(lags, (1, kernel))[:, : kernel * (2 * kernel - 1)]
    return flat.reshape(groups, kernel, 2 * kernel - 1)[:, :, kernel - 1 : 2 * kernel - 1]


def apply_blocks(matrix, blocks):
    return jnp.einsum("gts,bsgc->btgc", matrix, blocks, preferred_element_type=jnp.float32)


def body(outer_gate, inner_gate, stream, filters, query_rows, key_rows, *, rows, half):
    row_count, channels = outer_gate.shape
    groups, kernel = filters.shape
    group_size = channels // groups
    seq_span = 2 * half
    ctx_size = rows * half
    in_row = lax.axis_index("col") * CORES + lax.axis_index("core")
    row_index = lax.axis_index("row")
    shard_index = row_index * half + in_row
    seq_place = (shard_index + half) % seq_span
    product = (inner_gate.astype(jnp.float32) * stream.astype(jnp.float32)).astype(jnp.bfloat16)
    blocks = product.reshape(row_count // kernel, kernel, groups, group_size)
    near_taps = toeplitz_taps(filters, 0)
    far_taps = toeplitz_taps(filters, kernel)
    tail_rows = product[row_count - kernel + 1 :]
    earlier = passed_along(tail_rows, CTX_AXES, ctx_size, 1)
    earlier = jnp.where(seq_place == 0, jnp.zeros_like(earlier), earlier)
    first_block = jnp.concatenate([jnp.zeros((1, channels), jnp.bfloat16), earlier], 0)
    first_block = first_block.reshape(1, kernel, groups, group_size)
    before = jnp.concatenate([first_block, blocks[:-1]], 0)
    filtered = (apply_blocks(near_taps, blocks) + apply_blocks(far_taps, before)).reshape(
        row_count, channels
    )
    mixed = (outer_gate.astype(jnp.float32) * filtered).astype(jnp.bfloat16)
    local_heads = channels // HEAD_DIM
    queries = query_rows.reshape(row_count, local_heads, HEAD_DIM)
    score_scale = 1.0 / math.sqrt(HEAD_DIM)
    query_pos = shard_index * row_count + jnp.arange(row_count, dtype=jnp.int32)
    seq_start = jnp.maximum(shard_index - seq_place, 0) * row_count

    kv_rows = jnp.stack([key_rows, mixed])
    from_above = lax.ppermute(kv_rows, "row", [(r, r + 1) for r in range(rows - 1)])
    own_all = lax.all_gather(kv_rows, ("col", "core"), axis=0, tiled=False)
    above_all = lax.all_gather(from_above, ("col", "core"), axis=0, tiled=False)

    def attend(carried, gathered, source_row, first):
        weighted, row_peak, row_total = carried
        window = gathered[first : first + WINDOW_SHARDS]
        key_block = window[:, 0].reshape(WINDOW_SHARDS * row_count, local_heads, HEAD_DIM)
        value_block = window[:, 1].reshape(WINDOW_SHARDS * row_count, local_heads, HEAD_DIM)
        key_start = (source_row * half + first) * row_count
        key_pos = key_start + jnp.arange(WINDOW_SHARDS * row_count, dtype=jnp.int32)
        scores = (
            jnp.einsum("qhd,khd->hqk", queries, key_block, preferred_element_type=jnp.float32)
            * score_scale
        )
        visible_keys = (key_pos[None, :] >= seq_start) & (key_pos[None, :] <= query_pos[:, None])
        scores = jnp.where(visible_keys[None], scores, NEGATIVE)
        new_peak = jnp.maximum(row_peak, jnp.max(scores, axis=2))
        exp_terms = jnp.where(visible_keys[None], jnp.exp(scores - new_peak[..., None]), 0.0)
        rescale = jnp.exp(row_peak - new_peak)
        row_total = row_total * rescale + jnp.sum(exp_terms, axis=2)
        weights = exp_terms.astype(jnp.bfloat16)
        weighted = weighted * rescale[..., None] + jnp.einsum(
            "hqk,khd->hqd", weights, value_block, preferred_element_type=jnp.float32
        )
        return (weighted, new_peak, row_total)

    attn_state = (
        jnp.zeros((local_heads, row_count, HEAD_DIM), jnp.float32),
        jnp.full((local_heads, row_count), NEGATIVE, jnp.float32),
        jnp.zeros((local_heads, row_count), jnp.float32),
    )
    for gathered, source_row in ((own_all, row_index), (above_all, row_index - 1)):
        for first in range(0, half, WINDOW_SHARDS):
            attn_state = attend(attn_state, gathered, source_row, first)
    weighted, row_peak, row_total = attn_state
    attended = (
        (weighted / row_total[..., None])
        .transpose(1, 0, 2)
        .reshape(row_count, channels)
        .astype(jnp.bfloat16)
    )
    return (mixed, attended)


def solution(mesh):
    def run(outer_gate, inner_gate, stream, filters, query_rows, key_rows):
        ctx = mesh.shape["ctx"]
        row_count = outer_gate.shape[0] // ctx
        half = (LENGTH // 2) // row_count
        rows = ctx // half
        devices = mesh.devices.reshape(rows, half // CORES, CORES, mesh.shape["tp"])
        split = Mesh(devices, CTX_AXES + ("tp",))
        rows_spec = P(CTX_AXES, "tp")
        in_specs = (rows_spec, rows_spec, rows_spec, P("tp", None), rows_spec, rows_spec)
        outs = jax.shard_map(
            functools.partial(body, rows=rows, half=half),
            mesh=split,
            in_specs=in_specs,
            out_specs=(rows_spec, rows_spec),
            check_vma=False,
        )(outer_gate, inner_gate, stream, filters, query_rows, key_rows)
        placed = NamedSharding(mesh, P("ctx", "tp"))
        return tuple(lax.with_sharding_constraint(o, placed) for o in outs)

    return run
```

```python
import functools
import math

import jax
import jax.numpy as jnp
from jax import lax
from jax.sharding import Mesh, NamedSharding
from jax.sharding import PartitionSpec as P

HEAD_DIM = 128
LENGTH = 8192
CORES = 2
WINDOW_SHARDS = 8

NEGATIVE = -1e30
CTX_AXES = ("row", "col", "core")


def passed_along(block, axis, size, distance):
    route = [(i - distance, i) for i in range(size) if i - distance >= 0]
    return lax.ppermute(block, axis, route)


def toeplitz_taps(filters, offset):
    groups, kernel = filters.shape
    flipped = filters[:, ::-1]
    zeros = jnp.zeros_like(flipped)
    pieces = [flipped, zeros] if offset == 0 else [zeros, flipped]
    lags = jnp.concatenate(pieces, axis=1)
    flat = jnp.tile(lags, (1, kernel))[:, : kernel * (2 * kernel - 1)]
    return flat.reshape(groups, kernel, 2 * kernel - 1)[:, :, kernel - 1 : 2 * kernel - 1]


def apply_blocks(matrix, blocks):
    return jnp.einsum("gts,bsgc->btgc", matrix, blocks, preferred_element_type=jnp.float32)


def body(outer_gate, inner_gate, stream, filters, query_rows, key_rows, *, rows, half):
    row_count, channels = outer_gate.shape
    groups, kernel = filters.shape
    group_size = channels // groups
    seq_span = 2 * half
    ctx_size = rows * half
    in_row = lax.axis_index("col") * CORES + lax.axis_index("core")
    row_index = lax.axis_index("row")
    shard_index = row_index * half + in_row
    seq_place = (shard_index + half) % seq_span
    product = (inner_gate.astype(jnp.float32) * stream.astype(jnp.float32)).astype(jnp.bfloat16)
    blocks = product.reshape(row_count // kernel, kernel, groups, group_size)
    near_taps = toeplitz_taps(filters, 0)
    far_taps = toeplitz_taps(filters, kernel)
    tail_rows = product[row_count - kernel + 1 :]
    earlier = passed_along(tail_rows, CTX_AXES, ctx_size, 1)
    earlier = jnp.where(seq_place == 0, jnp.zeros_like(earlier), earlier)
    first_block = jnp.concatenate([jnp.zeros((1, channels), jnp.bfloat16), earlier], 0)
    first_block = first_block.reshape(1, kernel, groups, group_size)
    before = jnp.concatenate([first_block, blocks[:-1]], 0)
    filtered = (apply_blocks(near_taps, blocks) + apply_blocks(far_taps, before)).reshape(
        row_count, channels
    )
    mixed = (outer_gate.astype(jnp.float32) * filtered).astype(jnp.bfloat16)
    local_heads = channels // HEAD_DIM
    queries = query_rows.reshape(row_count, local_heads, HEAD_DIM)
    score_scale = 1.0 / math.sqrt(HEAD_DIM)
    query_pos = shard_index * row_count + jnp.arange(row_count, dtype=jnp.int32)
    seq_start = jnp.maximum(shard_index - seq_place, 0) * row_count

    def by_head(array):
        return array.reshape(row_count, local_heads, HEAD_DIM).transpose(1, 0, 2)

    def row_gather(array):
        return lax.all_gather(array, ("col", "core"), axis=1, tiled=True)

    def row_down(array):
        return lax.ppermute(array, "row", [(r, r + 1) for r in range(rows - 1)])

    head_queries = by_head(query_rows)
    head_keys = by_head(key_rows)
    head_values = by_head(mixed)
    keys_own = row_gather(head_keys)
    keys_above = row_gather(row_down(head_keys))
    values_own = row_gather(head_values)
    values_above = row_gather(row_down(head_values))
    window_rows = WINDOW_SHARDS * row_count

    def attend(carried, keys, values, source_row, first):
        weighted, row_peak, row_total = carried
        key_block = keys[:, first * row_count : first * row_count + window_rows]
        value_block = values[:, first * row_count : first * row_count + window_rows]
        key_start = (source_row * half + first) * row_count
        key_pos = key_start + jnp.arange(window_rows, dtype=jnp.int32)
        scores = (
            jnp.einsum("hqd,hkd->hqk", head_queries, key_block, preferred_element_type=jnp.float32)
            * score_scale
        )
        visible_keys = (key_pos[None, :] >= seq_start) & (key_pos[None, :] <= query_pos[:, None])
        scores = jnp.where(visible_keys[None], scores, NEGATIVE)
        new_peak = jnp.maximum(row_peak, jnp.max(scores, axis=2))
        exp_terms = jnp.where(visible_keys[None], jnp.exp(scores - new_peak[..., None]), 0.0)
        rescale = jnp.exp(row_peak - new_peak)
        row_total = row_total * rescale + jnp.sum(exp_terms, axis=2)
        weights = exp_terms.astype(jnp.bfloat16)
        weighted = weighted * rescale[..., None] + jnp.einsum(
            "hqk,hkd->hqd", weights, value_block, preferred_element_type=jnp.float32
        )
        return (weighted, new_peak, row_total)

    attn_state = (
        jnp.zeros((local_heads, row_count, HEAD_DIM), jnp.float32),
        jnp.full((local_heads, row_count), NEGATIVE, jnp.float32),
        jnp.zeros((local_heads, row_count), jnp.float32),
    )
    sources = ((keys_own, values_own, row_index), (keys_above, values_above, row_index - 1))
    for keys, values, source_row in sources:
        for first in range(0, half, WINDOW_SHARDS):
            attn_state = attend(attn_state, keys, values, source_row, first)
    weighted, row_peak, row_total = attn_state
    attended = (
        (weighted / row_total[..., None])
        .transpose(1, 0, 2)
        .reshape(row_count, channels)
        .astype(jnp.bfloat16)
    )
    return (mixed, attended)


def solution(mesh):
    def run(outer_gate, inner_gate, stream, filters, query_rows, key_rows):
        ctx = mesh.shape["ctx"]
        row_count = outer_gate.shape[0] // ctx
        half = (LENGTH // 2) // row_count
        rows = ctx // half
        devices = mesh.devices.reshape(rows, half // CORES, CORES, mesh.shape["tp"])
        split = Mesh(devices, CTX_AXES + ("tp",))
        rows_spec = P(CTX_AXES, "tp")
        in_specs = (rows_spec, rows_spec, rows_spec, P("tp", None), rows_spec, rows_spec)
        outs = jax.shard_map(
            functools.partial(body, rows=rows, half=half),
            mesh=split,
            in_specs=in_specs,
            out_specs=(rows_spec, rows_spec),
            check_vma=False,
        )(outer_gate, inner_gate, stream, filters, query_rows, key_rows)
        placed = NamedSharding(mesh, P("ctx", "tp"))
        return tuple(lax.with_sharding_constraint(o, placed) for o in outs)

    return run
```

```python
import functools
import math

import jax
import jax.numpy as jnp
from jax import lax
from jax.sharding import Mesh, NamedSharding
from jax.sharding import PartitionSpec as P

HEAD_DIM = 128
LENGTH = 8192
CORES = 2
WINDOW_SHARDS = 8

NEGATIVE = -1e30
CTX_AXES = ("row", "col", "core")


def passed_along(block, axis, size, distance):
    route = [(i - distance, i) for i in range(size) if i - distance >= 0]
    return lax.ppermute(block, axis, route)


def toeplitz_taps(filters, offset):
    groups, kernel = filters.shape
    flipped = filters[:, ::-1]
    zeros = jnp.zeros_like(flipped)
    pieces = [flipped, zeros] if offset == 0 else [zeros, flipped]
    lags = jnp.concatenate(pieces, axis=1)
    flat = jnp.tile(lags, (1, kernel))[:, : kernel * (2 * kernel - 1)]
    return flat.reshape(groups, kernel, 2 * kernel - 1)[:, :, kernel - 1 : 2 * kernel - 1]


def apply_blocks(matrix, blocks):
    return jnp.einsum("gts,bsgc->btgc", matrix, blocks, preferred_element_type=jnp.float32)


def body(outer_gate, inner_gate, stream, filters, query_rows, key_rows, *, rows, half):
    row_count, channels = outer_gate.shape
    groups, kernel = filters.shape
    group_size = channels // groups
    seq_span = 2 * half
    ctx_size = rows * half
    in_row = lax.axis_index("col") * CORES + lax.axis_index("core")
    row_index = lax.axis_index("row")
    shard_index = row_index * half + in_row
    seq_place = (shard_index + half) % seq_span
    product = (inner_gate.astype(jnp.float32) * stream.astype(jnp.float32)).astype(jnp.bfloat16)
    blocks = product.reshape(row_count // kernel, kernel, groups, group_size)
    near_taps = toeplitz_taps(filters, 0)
    far_taps = toeplitz_taps(filters, kernel)
    tail_rows = product[row_count - kernel + 1 :]
    earlier = passed_along(tail_rows, CTX_AXES, ctx_size, 1)
    earlier = jnp.where(seq_place == 0, jnp.zeros_like(earlier), earlier)
    first_block = jnp.concatenate([jnp.zeros((1, channels), jnp.bfloat16), earlier], 0)
    first_block = first_block.reshape(1, kernel, groups, group_size)
    before = jnp.concatenate([first_block, blocks[:-1]], 0)
    filtered = (apply_blocks(near_taps, blocks) + apply_blocks(far_taps, before)).reshape(
        row_count, channels
    )
    mixed = (outer_gate.astype(jnp.float32) * filtered).astype(jnp.bfloat16)
    local_heads = channels // HEAD_DIM
    queries = query_rows.reshape(row_count, local_heads, HEAD_DIM)
    score_scale = 1.0 / math.sqrt(HEAD_DIM)
    query_pos = shard_index * row_count + jnp.arange(row_count, dtype=jnp.int32)
    seq_start = jnp.maximum(shard_index - seq_place, 0) * row_count

    def row_down(array):
        return lax.ppermute(array, "row", [(r, r + 1) for r in range(rows - 1)])

    def row_gather(array):
        return lax.all_gather(jnp.stack([array, row_down(array)]), ("col", "core"), axis=0)

    keys_all = row_gather(key_rows)
    values_all = row_gather(mixed)
    window_rows = WINDOW_SHARDS * row_count
    windows = []
    for source, source_row in ((0, row_index), (1, row_index - 1)):
        for first in range(0, half, WINDOW_SHARDS):
            key_start = (source_row * half + first) * row_count
            key_pos = key_start + jnp.arange(window_rows, dtype=jnp.int32)
            visible = (key_pos[None, :] >= seq_start) & (key_pos[None, :] <= query_pos[:, None])
            keys = keys_all[first : first + WINDOW_SHARDS, source].reshape(window_rows, channels)
            values = values_all[first : first + WINDOW_SHARDS, source].reshape(window_rows, channels)
            windows.append((visible, keys, values))

    head_outputs = []
    for head in range(local_heads):
        lanes = slice(head * HEAD_DIM, (head + 1) * HEAD_DIM)
        head_queries = query_rows[:, lanes]
        weighted = jnp.zeros((row_count, HEAD_DIM), jnp.float32)
        row_peak = jnp.full((row_count, 1), NEGATIVE, jnp.float32)
        row_total = jnp.zeros((row_count, 1), jnp.float32)
        for visible, keys, values in windows:
            scores = (
                lax.dot_general(
                    head_queries,
                    keys[:, lanes],
                    (((1,), (1,)), ((), ())),
                    preferred_element_type=jnp.float32,
                )
                * score_scale
            )
            scores = jnp.where(visible, scores, NEGATIVE)
            new_peak = jnp.maximum(row_peak, jnp.max(scores, axis=1, keepdims=True))
            exp_terms = jnp.where(visible, jnp.exp(scores - new_peak), 0.0)
            rescale = jnp.exp(row_peak - new_peak)
            row_total = row_total * rescale + jnp.sum(exp_terms, axis=1, keepdims=True)
            weighted = weighted * rescale + jnp.dot(
                exp_terms.astype(jnp.bfloat16), values[:, lanes], preferred_element_type=jnp.float32
            )
            row_peak = new_peak
        head_outputs.append((weighted / row_total).astype(jnp.bfloat16))
    attended = jnp.concatenate(head_outputs, axis=1)
    return (mixed, attended)


def solution(mesh):
    def run(outer_gate, inner_gate, stream, filters, query_rows, key_rows):
        ctx = mesh.shape["ctx"]
        row_count = outer_gate.shape[0] // ctx
        half = (LENGTH // 2) // row_count
        rows = ctx // half
        devices = mesh.devices.reshape(rows, half // CORES, CORES, mesh.shape["tp"])
        split = Mesh(devices, CTX_AXES + ("tp",))
        rows_spec = P(CTX_AXES, "tp")
        in_specs = (rows_spec, rows_spec, rows_spec, P("tp", None), rows_spec, rows_spec)
        outs = jax.shard_map(
            functools.partial(body, rows=rows, half=half),
            mesh=split,
            in_specs=in_specs,
            out_specs=(rows_spec, rows_spec),
            check_vma=False,
        )(outer_gate, inner_gate, stream, filters, query_rows, key_rows)
        placed = NamedSharding(mesh, P("ctx", "tp"))
        return tuple(lax.with_sharding_constraint(o, placed) for o in outs)

    return run
```

```python
import functools
import math

import jax
import jax.numpy as jnp
from jax import lax
from jax.sharding import Mesh, NamedSharding
from jax.sharding import PartitionSpec as P

HEAD_DIM = 128
LENGTH = 8192
CORES = 2
WINDOW_SHARDS = 8

NEGATIVE = -1e30
CTX_AXES = ("row", "col", "core")


def passed_along(block, axis, size, distance):
    route = [(i - distance, i) for i in range(size) if i - distance >= 0]
    return lax.ppermute(block, axis, route)


def toeplitz_taps(filters, offset):
    groups, kernel = filters.shape
    flipped = filters[:, ::-1]
    zeros = jnp.zeros_like(flipped)
    pieces = [flipped, zeros] if offset == 0 else [zeros, flipped]
    lags = jnp.concatenate(pieces, axis=1)
    flat = jnp.tile(lags, (1, kernel))[:, : kernel * (2 * kernel - 1)]
    return flat.reshape(groups, kernel, 2 * kernel - 1)[:, :, kernel - 1 : 2 * kernel - 1]


def apply_blocks(matrix, blocks):
    return jnp.einsum("gts,bsgc->btgc", matrix, blocks, preferred_element_type=jnp.float32)


def body(outer_gate, inner_gate, stream, filters, query_rows, key_rows, *, rows, half):
    row_count, channels = outer_gate.shape
    groups, kernel = filters.shape
    group_size = channels // groups
    seq_span = 2 * half
    ctx_size = rows * half
    in_row = lax.axis_index("col") * CORES + lax.axis_index("core")
    row_index = lax.axis_index("row")
    shard_index = row_index * half + in_row
    seq_place = (shard_index + half) % seq_span
    product = (inner_gate.astype(jnp.float32) * stream.astype(jnp.float32)).astype(jnp.bfloat16)
    blocks = product.reshape(row_count // kernel, kernel, groups, group_size)
    near_taps = toeplitz_taps(filters, 0)
    far_taps = toeplitz_taps(filters, kernel)
    tail_rows = product[row_count - kernel + 1 :]
    earlier = passed_along(tail_rows, CTX_AXES, ctx_size, 1)
    earlier = jnp.where(seq_place == 0, jnp.zeros_like(earlier), earlier)
    first_block = jnp.concatenate([jnp.zeros((1, channels), jnp.bfloat16), earlier], 0)
    first_block = first_block.reshape(1, kernel, groups, group_size)
    before = jnp.concatenate([first_block, blocks[:-1]], 0)
    filtered = (apply_blocks(near_taps, blocks) + apply_blocks(far_taps, before)).reshape(
        row_count, channels
    )
    mixed = (outer_gate.astype(jnp.float32) * filtered).astype(jnp.bfloat16)
    local_heads = channels // HEAD_DIM
    queries = query_rows.reshape(row_count, local_heads, HEAD_DIM)
    score_scale = 1.0 / math.sqrt(HEAD_DIM)
    query_pos = shard_index * row_count + jnp.arange(row_count, dtype=jnp.int32)
    seq_start = jnp.maximum(shard_index - seq_place, 0) * row_count

    def row_down(array):
        return lax.ppermute(array, "row", [(r, r + 1) for r in range(rows - 1)])

    def row_gather(array):
        return lax.all_gather(jnp.stack([array, row_down(array)]), ("col", "core"), axis=0)

    keys_all = row_gather(key_rows)
    values_all = row_gather(mixed)
    gathered_rows = keys_all.shape[0] * keys_all.shape[1] * row_count
    keys_all = keys_all.reshape(gathered_rows, channels)
    values_all = values_all.reshape(gathered_rows, channels)
    key_index = jnp.arange(gathered_rows, dtype=jnp.int32)
    key_shard = key_index // (2 * row_count)
    key_source = (key_index // row_count) % 2
    key_pos = ((row_index - key_source) * half + key_shard) * row_count + key_index % row_count
    visible = (key_pos[None, :] >= seq_start) & (key_pos[None, :] <= query_pos[:, None])

    head_outputs = []
    for head in range(local_heads):
        lanes = slice(head * HEAD_DIM, (head + 1) * HEAD_DIM)
        scores = (
            lax.dot_general(
                query_rows[:, lanes],
                keys_all[:, lanes],
                (((1,), (1,)), ((), ())),
                preferred_element_type=jnp.float32,
            )
            * score_scale
        )
        scores = jnp.where(visible, scores, NEGATIVE)
        row_peak = jnp.max(scores, axis=1, keepdims=True)
        exp_terms = jnp.where(visible, jnp.exp(scores - row_peak), 0.0)
        row_total = jnp.sum(exp_terms, axis=1, keepdims=True)
        weighted = jnp.dot(
            exp_terms.astype(jnp.bfloat16), values_all[:, lanes], preferred_element_type=jnp.float32
        )
        head_outputs.append((weighted / row_total).astype(jnp.bfloat16))
    attended = jnp.concatenate(head_outputs, axis=1)
    return (mixed, attended)


def solution(mesh):
    def run(outer_gate, inner_gate, stream, filters, query_rows, key_rows):
        ctx = mesh.shape["ctx"]
        row_count = outer_gate.shape[0] // ctx
        half = (LENGTH // 2) // row_count
        rows = ctx // half
        devices = mesh.devices.reshape(rows, half // CORES, CORES, mesh.shape["tp"])
        split = Mesh(devices, CTX_AXES + ("tp",))
        rows_spec = P(CTX_AXES, "tp")
        in_specs = (rows_spec, rows_spec, rows_spec, P("tp", None), rows_spec, rows_spec)
        outs = jax.shard_map(
            functools.partial(body, rows=rows, half=half),
            mesh=split,
            in_specs=in_specs,
            out_specs=(rows_spec, rows_spec),
            check_vma=False,
        )(outer_gate, inner_gate, stream, filters, query_rows, key_rows)
        placed = NamedSharding(mesh, P("ctx", "tp"))
        return tuple(lax.with_sharding_constraint(o, placed) for o in outs)

    return run
```

```python
import functools
import math

import jax
import jax.numpy as jnp
from jax import lax
from jax.sharding import Mesh, NamedSharding
from jax.sharding import PartitionSpec as P

HEAD_DIM = 128
LENGTH = 8192
CORES = 2
WINDOW_SHARDS = 8

NEGATIVE = -1e30
CTX_AXES = ("row", "col", "core")


def passed_along(block, axis, size, distance):
    route = [(i - distance, i) for i in range(size) if i - distance >= 0]
    return lax.ppermute(block, axis, route)


def toeplitz_taps(filters, offset):
    groups, kernel = filters.shape
    flipped = filters[:, ::-1]
    zeros = jnp.zeros_like(flipped)
    pieces = [flipped, zeros] if offset == 0 else [zeros, flipped]
    lags = jnp.concatenate(pieces, axis=1)
    flat = jnp.tile(lags, (1, kernel))[:, : kernel * (2 * kernel - 1)]
    return flat.reshape(groups, kernel, 2 * kernel - 1)[:, :, kernel - 1 : 2 * kernel - 1]


def apply_blocks(matrix, blocks):
    return jnp.einsum("gts,bsgc->btgc", matrix, blocks, preferred_element_type=jnp.float32)


def body(outer_gate, inner_gate, stream, filters, query_rows, key_rows, *, rows, half):
    row_count, channels = outer_gate.shape
    groups, kernel = filters.shape
    group_size = channels // groups
    seq_span = 2 * half
    ctx_size = rows * half
    in_row = lax.axis_index("col") * CORES + lax.axis_index("core")
    row_index = lax.axis_index("row")
    shard_index = row_index * half + in_row
    seq_place = (shard_index + half) % seq_span
    product = (inner_gate.astype(jnp.float32) * stream.astype(jnp.float32)).astype(jnp.bfloat16)
    blocks = product.reshape(row_count // kernel, kernel, groups, group_size)
    near_taps = toeplitz_taps(filters, 0)
    far_taps = toeplitz_taps(filters, kernel)
    tail_rows = product[row_count - kernel + 1 :]
    earlier = passed_along(tail_rows, CTX_AXES, ctx_size, 1)
    earlier = jnp.where(seq_place == 0, jnp.zeros_like(earlier), earlier)
    first_block = jnp.concatenate([jnp.zeros((1, channels), jnp.bfloat16), earlier], 0)
    first_block = first_block.reshape(1, kernel, groups, group_size)
    before = jnp.concatenate([first_block, blocks[:-1]], 0)
    filtered = (apply_blocks(near_taps, blocks) + apply_blocks(far_taps, before)).reshape(
        row_count, channels
    )
    mixed = (outer_gate.astype(jnp.float32) * filtered).astype(jnp.bfloat16)
    local_heads = channels // HEAD_DIM
    queries = query_rows.reshape(row_count, local_heads, HEAD_DIM)
    score_scale = 1.0 / math.sqrt(HEAD_DIM)
    query_pos = shard_index * row_count + jnp.arange(row_count, dtype=jnp.int32)
    seq_start = jnp.maximum(shard_index - seq_place, 0) * row_count

    def row_down(array):
        return lax.ppermute(array, "row", [(r, r + 1) for r in range(rows - 1)])

    def row_gather(array):
        pair = jnp.stack([array, row_down(array)])
        mine = lax.all_gather(pair, "col", axis=0)
        other = lax.ppermute(mine, "core", [(c, (c + 1) % CORES) for c in range(CORES)])
        return mine, other

    keys_mine, keys_other = row_gather(key_rows)
    values_mine, values_other = row_gather(mixed)
    core_index = lax.axis_index("core")
    halves = []
    for keys, values, core_of in (
        (keys_mine, values_mine, core_index),
        (keys_other, values_other, (core_index + 1) % CORES),
    ):
        gathered_rows = keys.shape[0] * keys.shape[1] * row_count
        key_index = jnp.arange(gathered_rows, dtype=jnp.int32)
        key_col = key_index // (2 * row_count)
        key_source = (key_index // row_count) % 2
        key_shard = key_col * CORES + core_of
        key_pos = ((row_index - key_source) * half + key_shard) * row_count + key_index % row_count
        visible = (key_pos[None, :] >= seq_start) & (key_pos[None, :] <= query_pos[:, None])
        halves.append(
            (visible, keys.reshape(gathered_rows, channels), values.reshape(gathered_rows, channels))
        )

    head_outputs = []
    for head in range(local_heads):
        lanes = slice(head * HEAD_DIM, (head + 1) * HEAD_DIM)
        scored = []
        for visible, keys, values in halves:
            scores = (
                lax.dot_general(
                    query_rows[:, lanes],
                    keys[:, lanes],
                    (((1,), (1,)), ((), ())),
                    preferred_element_type=jnp.float32,
                )
                * score_scale
            )
            scored.append(jnp.where(visible, scores, NEGATIVE))
        row_peak = jnp.maximum(
            jnp.max(scored[0], axis=1, keepdims=True), jnp.max(scored[1], axis=1, keepdims=True)
        )
        row_total = jnp.zeros((row_count, 1), jnp.float32)
        weighted = jnp.zeros((row_count, HEAD_DIM), jnp.float32)
        for scores, (visible, keys, values) in zip(scored, halves):
            exp_terms = jnp.where(visible, jnp.exp(scores - row_peak), 0.0)
            row_total = row_total + jnp.sum(exp_terms, axis=1, keepdims=True)
            weighted = weighted + jnp.dot(
                exp_terms.astype(jnp.bfloat16), values[:, lanes], preferred_element_type=jnp.float32
            )
        head_outputs.append((weighted / row_total).astype(jnp.bfloat16))
    attended = jnp.concatenate(head_outputs, axis=1)
    return (mixed, attended)


def solution(mesh):
    def run(outer_gate, inner_gate, stream, filters, query_rows, key_rows):
        ctx = mesh.shape["ctx"]
        row_count = outer_gate.shape[0] // ctx
        half = (LENGTH // 2) // row_count
        rows = ctx // half
        devices = mesh.devices.reshape(rows, half // CORES, CORES, mesh.shape["tp"])
        split = Mesh(devices, CTX_AXES + ("tp",))
        rows_spec = P(CTX_AXES, "tp")
        in_specs = (rows_spec, rows_spec, rows_spec, P("tp", None), rows_spec, rows_spec)
        outs = jax.shard_map(
            functools.partial(body, rows=rows, half=half),
            mesh=split,
            in_specs=in_specs,
            out_specs=(rows_spec, rows_spec),
            check_vma=False,
        )(outer_gate, inner_gate, stream, filters, query_rows, key_rows)
        placed = NamedSharding(mesh, P("ctx", "tp"))
        return tuple(lax.with_sharding_constraint(o, placed) for o in outs)

    return run
```

```python
import functools
import math

import jax
import jax.numpy as jnp
from jax import lax
from jax.sharding import Mesh, NamedSharding
from jax.sharding import PartitionSpec as P

HEAD_DIM = 128
LENGTH = 8192
CORES = 2
WINDOW_SHARDS = 8

NEGATIVE = -1e30
CTX_AXES = ("row", "col", "core")


def passed_along(block, axis, size, distance):
    route = [(i - distance, i) for i in range(size) if i - distance >= 0]
    return lax.ppermute(block, axis, route)


def toeplitz_taps(filters, offset):
    groups, kernel = filters.shape
    flipped = filters[:, ::-1]
    zeros = jnp.zeros_like(flipped)
    pieces = [flipped, zeros] if offset == 0 else [zeros, flipped]
    lags = jnp.concatenate(pieces, axis=1)
    flat = jnp.tile(lags, (1, kernel))[:, : kernel * (2 * kernel - 1)]
    return flat.reshape(groups, kernel, 2 * kernel - 1)[:, :, kernel - 1 : 2 * kernel - 1]


def apply_blocks(matrix, blocks):
    return jnp.einsum("gts,bsgc->btgc", matrix, blocks, preferred_element_type=jnp.float32)


def body(outer_gate, inner_gate, stream, filters, query_rows, key_rows, *, rows, half):
    row_count, channels = outer_gate.shape
    groups, kernel = filters.shape
    group_size = channels // groups
    seq_span = 2 * half
    ctx_size = rows * half
    in_row = lax.axis_index("col") * CORES + lax.axis_index("core")
    row_index = lax.axis_index("row")
    shard_index = row_index * half + in_row
    seq_place = (shard_index + half) % seq_span
    cols = half // CORES
    ahead = [(i, (i + 1) % cols) for i in range(cols)]
    behind = [(i, (i - 1) % cols) for i in range(cols)]
    swap = [(c, (c + 1) % CORES) for c in range(CORES)]

    def row_down(array):
        return lax.ppermute(array, "row", [(r, r + 1) for r in range(rows - 1)])

    def row_gather(array, tied=()):
        tied = list(tied)
        pair = jnp.stack([array, row_down(array)])
        pieces = [pair]
        forward = backward = pair
        for step in range(1, cols // 2):
            forward = lax.ppermute(forward, "col", ahead)
            backward = lax.ppermute(backward, "col", behind)
            if tied:
                item = tied.pop(0)
                item = item() if callable(item) else item
                forward, backward, released = lax.optimization_barrier((forward, backward, item))
                released_stages.append(released)
            pieces += [forward, backward]
        last_own = lax.ppermute(forward[0], "col", ahead)
        last_above = lax.ppermute(backward[1], "col", behind)
        pieces.append(jnp.stack([last_own, last_above]))
        mine = jnp.stack(pieces)
        return mine, lax.ppermute(mine, "core", swap)

    released_stages = []
    keys_mine, keys_other = row_gather(key_rows, tied=[filters, filters, outer_gate])
    filters_near, filters_far, outer_gate = released_stages

    product = (inner_gate.astype(jnp.float32) * stream.astype(jnp.float32)).astype(jnp.bfloat16)
    blocks = product.reshape(row_count // kernel, kernel, groups, group_size)
    near_taps = toeplitz_taps(filters_near, 0)
    far_taps = toeplitz_taps(filters_far, kernel)
    tail_rows = product[row_count - kernel + 1 :]
    earlier = passed_along(tail_rows, CTX_AXES, ctx_size, 1)
    earlier = jnp.where(seq_place == 0, jnp.zeros_like(earlier), earlier)
    first_block = jnp.concatenate([jnp.zeros((1, channels), jnp.bfloat16), earlier], 0)
    first_block = first_block.reshape(1, kernel, groups, group_size)
    before = jnp.concatenate([first_block, blocks[:-1]], 0)
    filtered = (apply_blocks(near_taps, blocks) + apply_blocks(far_taps, before)).reshape(
        row_count, channels
    )
    mixed = (outer_gate.astype(jnp.float32) * filtered).astype(jnp.bfloat16)
    local_heads = channels // HEAD_DIM
    queries = query_rows.reshape(row_count, local_heads, HEAD_DIM)
    score_scale = 1.0 / math.sqrt(HEAD_DIM)
    query_pos = shard_index * row_count + jnp.arange(row_count, dtype=jnp.int32)
    seq_start = jnp.maximum(shard_index - seq_place, 0) * row_count

    core_index = lax.axis_index("core")
    col_index = lax.axis_index("col")

    def key_visibility(core_of):
        gathered_rows = cols * 2 * row_count
        key_index = jnp.arange(gathered_rows, dtype=jnp.int32)
        piece = key_index // (2 * row_count)
        reach = (piece + 1) // 2
        offset = jnp.where(piece % 2 == 1, -reach, reach)
        key_col = (col_index + offset + cols) % cols
        key_source = (key_index // row_count) % 2
        key_shard = key_col * CORES + core_of
        key_pos = ((row_index - key_source) * half + key_shard) * row_count + key_index % row_count
        return (key_pos[None, :] >= seq_start) & (key_pos[None, :] <= query_pos[:, None])

    half_keys = (
        (key_visibility(core_index), keys_mine.reshape(-1, channels)),
        (key_visibility((core_index + 1) % CORES), keys_other.reshape(-1, channels)),
    )
    def head_softmax(head, head_queries):
        lanes = slice(head * HEAD_DIM, (head + 1) * HEAD_DIM)
        scored = []
        for visible, keys in half_keys:
            scores = (
                lax.dot_general(
                    head_queries,
                    keys[:, lanes],
                    (((1,), (1,)), ((), ())),
                    preferred_element_type=jnp.float32,
                )
                * score_scale
            )
            scored.append(jnp.where(visible, scores, NEGATIVE))
        row_peak = jnp.maximum(
            jnp.max(scored[0], axis=1, keepdims=True), jnp.max(scored[1], axis=1, keepdims=True)
        )
        row_total = jnp.zeros((row_count, 1), jnp.float32)
        weights = []
        for scores, (visible, keys) in zip(scored, half_keys):
            exp_terms = jnp.where(visible, jnp.exp(scores - row_peak), 0.0)
            row_total = row_total + jnp.sum(exp_terms, axis=1, keepdims=True)
            weights.append(exp_terms.astype(jnp.bfloat16))
        return (tuple(weights), row_total)

    def head_queries(head):
        return query_rows[:, head * HEAD_DIM : (head + 1) * HEAD_DIM]

    head_results = [head_softmax(0, head_queries(0))]

    def take_released():
        finished, queries_now = released_stages[-1]
        head_results[len(head_results) - 1] = finished
        head_results.append(head_softmax(len(head_results), queries_now))

    def next_head(head):
        def tie():
            if head >= 2:
                take_released()
            return (head_results[head - 1], head_queries(head))

        return tie

    released_stages = []
    ring_rounds = cols // 2 - 1
    values_mine, values_other = row_gather(
        mixed, tied=[next_head(head) for head in range(1, min(local_heads, ring_rounds + 1))]
    )
    if released_stages:
        take_released()
    for head in range(len(head_results), local_heads):
        head_results.append(head_softmax(head, head_queries(head)))
    head_weights = [weights for weights, total in head_results]
    head_totals = [total for weights, total in head_results]
    half_values = (values_mine.reshape(-1, channels), values_other.reshape(-1, channels))

    head_outputs = []
    for head in range(local_heads):
        lanes = slice(head * HEAD_DIM, (head + 1) * HEAD_DIM)
        weighted = jnp.zeros((row_count, HEAD_DIM), jnp.float32)
        for weights, values in zip(head_weights[head], half_values):
            weighted = weighted + jnp.dot(weights, values[:, lanes], preferred_element_type=jnp.float32)
        head_outputs.append((weighted / head_totals[head]).astype(jnp.bfloat16))
    attended = jnp.concatenate(head_outputs, axis=1)
    return (mixed, attended)


def solution(mesh):
    def run(outer_gate, inner_gate, stream, filters, query_rows, key_rows):
        ctx = mesh.shape["ctx"]
        row_count = outer_gate.shape[0] // ctx
        half = (LENGTH // 2) // row_count
        rows = ctx // half
        devices = mesh.devices.reshape(rows, half // CORES, CORES, mesh.shape["tp"])
        split = Mesh(devices, CTX_AXES + ("tp",))
        rows_spec = P(CTX_AXES, "tp")
        in_specs = (rows_spec, rows_spec, rows_spec, P("tp", None), rows_spec, rows_spec)
        outs = jax.shard_map(
            functools.partial(body, rows=rows, half=half),
            mesh=split,
            in_specs=in_specs,
            out_specs=(rows_spec, rows_spec),
            check_vma=False,
        )(outer_gate, inner_gate, stream, filters, query_rows, key_rows)
        placed = NamedSharding(mesh, P("ctx", "tp"))
        return tuple(lax.with_sharding_constraint(o, placed) for o in outs)

    return run
```

```python
import functools
import math

import jax
import jax.numpy as jnp
from jax import lax
from jax.sharding import Mesh, NamedSharding
from jax.sharding import PartitionSpec as P

HEAD_DIM = 128
LENGTH = 8192
CORES = 2
WINDOW_SHARDS = 8

NEGATIVE = -1e30
CTX_AXES = ("row", "col", "core")


def passed_along(block, axis, size, distance):
    route = [(i - distance, i) for i in range(size) if i - distance >= 0]
    return lax.ppermute(block, axis, route)


def toeplitz_taps(filters, offset):
    groups, kernel = filters.shape
    flipped = filters[:, ::-1]
    zeros = jnp.zeros_like(flipped)
    pieces = [flipped, zeros] if offset == 0 else [zeros, flipped]
    lags = jnp.concatenate(pieces, axis=1)
    flat = jnp.tile(lags, (1, kernel))[:, : kernel * (2 * kernel - 1)]
    return flat.reshape(groups, kernel, 2 * kernel - 1)[:, :, kernel - 1 : 2 * kernel - 1]


def apply_blocks(matrix, blocks):
    return jnp.einsum("gts,bsgc->btgc", matrix, blocks, preferred_element_type=jnp.float32)


def body(outer_gate, inner_gate, stream, filters, query_rows, key_rows, *, rows, half):
    row_count, channels = outer_gate.shape
    groups, kernel = filters.shape
    group_size = channels // groups
    seq_span = 2 * half
    ctx_size = rows * half
    in_row = lax.axis_index("col") * CORES + lax.axis_index("core")
    row_index = lax.axis_index("row")
    shard_index = row_index * half + in_row
    seq_place = (shard_index + half) % seq_span
    product = (inner_gate.astype(jnp.float32) * stream.astype(jnp.float32)).astype(jnp.bfloat16)
    blocks = product.reshape(row_count // kernel, kernel, groups, group_size)
    near_taps = toeplitz_taps(filters, 0)
    far_taps = toeplitz_taps(filters, kernel)
    tail_rows = product[row_count - kernel + 1 :]
    earlier = passed_along(tail_rows, CTX_AXES, ctx_size, 1)
    earlier = jnp.where(seq_place == 0, jnp.zeros_like(earlier), earlier)
    first_block = jnp.concatenate([jnp.zeros((1, channels), jnp.bfloat16), earlier], 0)
    first_block = first_block.reshape(1, kernel, groups, group_size)
    before = jnp.concatenate([first_block, blocks[:-1]], 0)
    filtered = (apply_blocks(near_taps, blocks) + apply_blocks(far_taps, before)).reshape(
        row_count, channels
    )
    mixed = (outer_gate.astype(jnp.float32) * filtered).astype(jnp.bfloat16)
    local_heads = channels // HEAD_DIM
    queries = query_rows.reshape(row_count, local_heads, HEAD_DIM)
    score_scale = 1.0 / math.sqrt(HEAD_DIM)
    query_pos = shard_index * row_count + jnp.arange(row_count, dtype=jnp.int32)
    seq_start = jnp.maximum(shard_index - seq_place, 0) * row_count

    def row_down(array):
        return lax.ppermute(array, "row", [(r, r + 1) for r in range(rows - 1)])

    def row_gather(array):
        return lax.all_gather(jnp.stack([array, row_down(array)]), ("col", "core"), axis=0)

    keys_all = row_gather(key_rows)
    values_all = row_gather(mixed)
    gathered_rows = keys_all.shape[0] * keys_all.shape[1] * row_count
    keys_all = keys_all.reshape(gathered_rows, channels)
    values_all = values_all.reshape(gathered_rows, channels)
    key_index = jnp.arange(gathered_rows, dtype=jnp.int32)
    key_shard = key_index // (2 * row_count)
    key_source = (key_index // row_count) % 2
    key_pos = ((row_index - key_source) * half + key_shard) * row_count + key_index % row_count
    visible = (key_pos[None, :] >= seq_start) & (key_pos[None, :] <= query_pos[:, None])

    head_outputs = []
    for head in range(local_heads):
        lanes = slice(head * HEAD_DIM, (head + 1) * HEAD_DIM)
        scores = (
            lax.dot_general(
                query_rows[:, lanes],
                keys_all[:, lanes],
                (((1,), (1,)), ((), ())),
                preferred_element_type=jnp.float32,
            )
            * score_scale
        )
        scores = jnp.where(visible, scores, NEGATIVE)
        row_peak = jnp.max(scores, axis=1, keepdims=True)
        exp_terms = jnp.where(visible, jnp.exp(scores - row_peak), 0.0)
        row_total = jnp.sum(exp_terms, axis=1, keepdims=True)
        weights, row_total = lax.optimization_barrier((exp_terms.astype(jnp.bfloat16), row_total))
        weighted = jnp.dot(weights, values_all[:, lanes], preferred_element_type=jnp.float32)
        head_outputs.append((weighted / row_total).astype(jnp.bfloat16))
    attended = jnp.concatenate(head_outputs, axis=1)
    return (mixed, attended)


def solution(mesh):
    def run(outer_gate, inner_gate, stream, filters, query_rows, key_rows):
        ctx = mesh.shape["ctx"]
        row_count = outer_gate.shape[0] // ctx
        half = (LENGTH // 2) // row_count
        rows = ctx // half
        devices = mesh.devices.reshape(rows, half // CORES, CORES, mesh.shape["tp"])
        split = Mesh(devices, CTX_AXES + ("tp",))
        rows_spec = P(CTX_AXES, "tp")
        in_specs = (rows_spec, rows_spec, rows_spec, P("tp", None), rows_spec, rows_spec)
        outs = jax.shard_map(
            functools.partial(body, rows=rows, half=half),
            mesh=split,
            in_specs=in_specs,
            out_specs=(rows_spec, rows_spec),
            check_vma=False,
        )(outer_gate, inner_gate, stream, filters, query_rows, key_rows)
        placed = NamedSharding(mesh, P("ctx", "tp"))
        return tuple(lax.with_sharding_constraint(o, placed) for o in outs)

    return run
```

```python
import functools
import math

import jax
import jax.numpy as jnp
from jax import lax
from jax.sharding import Mesh, NamedSharding
from jax.sharding import PartitionSpec as P

HEAD_DIM = 128
LENGTH = 8192
CORES = 2
WINDOW_SHARDS = 8

NEGATIVE = -1e30
CTX_AXES = ("row", "col", "core")


def passed_along(block, axis, size, distance):
    route = [(i - distance, i) for i in range(size) if i - distance >= 0]
    return lax.ppermute(block, axis, route)


def toeplitz_taps(filters, offset):
    groups, kernel = filters.shape
    lag = jnp.arange(kernel, dtype=jnp.int32)[:, None, None]
    out_row = jnp.arange(kernel, dtype=jnp.int32)[None, :, None]
    in_row = jnp.arange(kernel, dtype=jnp.int32)[None, None, :]
    picks = (out_row - in_row + offset == lag).astype(filters.dtype).reshape(kernel, kernel * kernel)
    taps = jnp.dot(filters, picks, preferred_element_type=jnp.float32)
    return taps.astype(filters.dtype).reshape(groups, kernel, kernel)


def apply_blocks(matrix, blocks):
    return jnp.einsum("gts,bsgc->btgc", matrix, blocks, preferred_element_type=jnp.float32)


def body(outer_gate, inner_gate, stream, filters, query_rows, key_rows, *, rows, half):
    row_count, channels = outer_gate.shape
    groups, kernel = filters.shape
    group_size = channels // groups
    seq_span = 2 * half
    ctx_size = rows * half
    in_row = lax.axis_index("col") * CORES + lax.axis_index("core")
    row_index = lax.axis_index("row")
    shard_index = row_index * half + in_row
    seq_place = (shard_index + half) % seq_span
    product = (inner_gate.astype(jnp.float32) * stream.astype(jnp.float32)).astype(jnp.bfloat16)
    blocks = product.reshape(row_count // kernel, kernel, groups, group_size)
    near_taps = toeplitz_taps(filters, 0)
    far_taps = toeplitz_taps(filters, kernel)
    tail_rows = product[row_count - kernel + 1 :]
    earlier = passed_along(tail_rows, CTX_AXES, ctx_size, 1)
    earlier = jnp.where(seq_place == 0, jnp.zeros_like(earlier), earlier)
    first_block = jnp.concatenate([jnp.zeros((1, channels), jnp.bfloat16), earlier], 0)
    first_block = first_block.reshape(1, kernel, groups, group_size)
    before = jnp.concatenate([first_block, blocks[:-1]], 0)
    filtered = (apply_blocks(near_taps, blocks) + apply_blocks(far_taps, before)).reshape(
        row_count, channels
    )
    mixed = (outer_gate.astype(jnp.float32) * filtered).astype(jnp.bfloat16)
    local_heads = channels // HEAD_DIM
    queries = query_rows.reshape(row_count, local_heads, HEAD_DIM)
    score_scale = 1.0 / math.sqrt(HEAD_DIM)
    query_pos = shard_index * row_count + jnp.arange(row_count, dtype=jnp.int32)
    seq_start = jnp.maximum(shard_index - seq_place, 0) * row_count

    def row_down(array):
        return lax.ppermute(array, "row", [(r, r + 1) for r in range(rows - 1)])

    def row_gather(array):
        return lax.all_gather(jnp.stack([array, row_down(array)]), ("col", "core"), axis=0)

    keys_all = row_gather(key_rows)
    values_all = row_gather(mixed)
    gathered_rows = keys_all.shape[0] * keys_all.shape[1] * row_count
    keys_all = keys_all.reshape(gathered_rows, channels)
    values_all = values_all.reshape(gathered_rows, channels)
    key_index = jnp.arange(gathered_rows, dtype=jnp.int32)
    key_shard = key_index // (2 * row_count)
    key_source = (key_index // row_count) % 2
    key_pos = ((row_index - key_source) * half + key_shard) * row_count + key_index % row_count
    visible = (key_pos[None, :] >= seq_start) & (key_pos[None, :] <= query_pos[:, None])

    head_outputs = []
    for head in range(local_heads):
        lanes = slice(head * HEAD_DIM, (head + 1) * HEAD_DIM)
        scores = (
            lax.dot_general(
                query_rows[:, lanes],
                keys_all[:, lanes],
                (((1,), (1,)), ((), ())),
                preferred_element_type=jnp.float32,
            )
            * score_scale
        )
        scores = jnp.where(visible, scores, NEGATIVE)
        row_peak = jnp.max(scores, axis=1, keepdims=True)
        exp_terms = jnp.where(visible, jnp.exp(scores - row_peak), 0.0)
        row_total = jnp.sum(exp_terms, axis=1, keepdims=True)
        weights, row_total = lax.optimization_barrier((exp_terms.astype(jnp.bfloat16), row_total))
        weighted = jnp.dot(weights, values_all[:, lanes], preferred_element_type=jnp.float32)
        head_outputs.append((weighted / row_total).astype(jnp.bfloat16))
    attended = jnp.concatenate(head_outputs, axis=1)
    return (mixed, attended)


def solution(mesh):
    def run(outer_gate, inner_gate, stream, filters, query_rows, key_rows):
        ctx = mesh.shape["ctx"]
        row_count = outer_gate.shape[0] // ctx
        half = (LENGTH // 2) // row_count
        rows = ctx // half
        devices = mesh.devices.reshape(rows, half // CORES, CORES, mesh.shape["tp"])
        split = Mesh(devices, CTX_AXES + ("tp",))
        rows_spec = P(CTX_AXES, "tp")
        in_specs = (rows_spec, rows_spec, rows_spec, P("tp", None), rows_spec, rows_spec)
        outs = jax.shard_map(
            functools.partial(body, rows=rows, half=half),
            mesh=split,
            in_specs=in_specs,
            out_specs=(rows_spec, rows_spec),
            check_vma=False,
        )(outer_gate, inner_gate, stream, filters, query_rows, key_rows)
        placed = NamedSharding(mesh, P("ctx", "tp"))
        return tuple(lax.with_sharding_constraint(o, placed) for o in outs)

    return run
```

```python
import functools
import math

import jax
import jax.numpy as jnp
from jax import lax
from jax.sharding import Mesh, NamedSharding
from jax.sharding import PartitionSpec as P

HEAD_DIM = 128
LENGTH = 8192
CORES = 2
WINDOW_SHARDS = 8

NEGATIVE = -1e30
CTX_AXES = ("row", "col", "core")


def passed_along(block, axis, size, distance):
    route = [(i - distance, i) for i in range(size) if i - distance >= 0]
    return lax.ppermute(block, axis, route)


def toeplitz_taps(filters, offset):
    groups, kernel = filters.shape
    lag = jnp.arange(kernel, dtype=jnp.int32)[:, None, None]
    out_row = jnp.arange(kernel, dtype=jnp.int32)[None, :, None]
    in_row = jnp.arange(kernel, dtype=jnp.int32)[None, None, :]
    picks = (out_row - in_row + offset == lag).astype(filters.dtype).reshape(kernel, kernel * kernel)
    taps = jnp.dot(filters, picks, preferred_element_type=jnp.float32)
    return taps.astype(filters.dtype).reshape(groups, kernel, kernel)


def apply_blocks(matrix, blocks):
    return jnp.einsum("gts,bsgc->btgc", matrix, blocks, preferred_element_type=jnp.float32)


def body(outer_gate, inner_gate, stream, filters, query_rows, key_rows, *, rows, half):
    row_count, channels = outer_gate.shape
    groups, kernel = filters.shape
    group_size = channels // groups
    seq_span = 2 * half
    ctx_size = rows * half
    in_row = lax.axis_index("col") * CORES + lax.axis_index("core")
    row_index = lax.axis_index("row")
    shard_index = row_index * half + in_row
    seq_place = (shard_index + half) % seq_span
    product = (inner_gate.astype(jnp.float32) * stream.astype(jnp.float32)).astype(jnp.bfloat16)
    blocks = product.reshape(row_count // kernel, kernel, groups, group_size)
    near_taps = toeplitz_taps(filters, 0)
    far_taps = toeplitz_taps(filters, kernel)
    tail_rows = product[row_count - kernel + 1 :]
    earlier = passed_along(tail_rows, CTX_AXES, ctx_size, 1)
    earlier = jnp.where(seq_place == 0, jnp.zeros_like(earlier), earlier)
    first_block = jnp.concatenate([jnp.zeros((1, channels), jnp.bfloat16), earlier], 0)
    first_block = first_block.reshape(1, kernel, groups, group_size)
    before = jnp.concatenate([first_block, blocks[:-1]], 0)
    filtered = (apply_blocks(near_taps, blocks) + apply_blocks(far_taps, before)).reshape(
        row_count, channels
    )
    mixed = (outer_gate.astype(jnp.float32) * filtered).astype(jnp.bfloat16)
    local_heads = channels // HEAD_DIM
    queries = query_rows.reshape(row_count, local_heads, HEAD_DIM)
    score_scale = 1.0 / math.sqrt(HEAD_DIM)
    query_pos = shard_index * row_count + jnp.arange(row_count, dtype=jnp.int32)
    seq_start = jnp.maximum(shard_index - seq_place, 0) * row_count

    def row_down(array):
        return lax.ppermute(array, "row", [(r, r + 1) for r in range(rows - 1)])

    def row_gather(array):
        return lax.all_gather(jnp.stack([array, row_down(array)]), ("col", "core"), axis=0)

    both_all = row_gather(jnp.concatenate([key_rows, mixed], axis=1))
    keys_all = both_all[..., :channels]
    values_all = both_all[..., channels:]
    gathered_rows = keys_all.shape[0] * keys_all.shape[1] * row_count
    keys_all = keys_all.reshape(gathered_rows, channels)
    values_all = values_all.reshape(gathered_rows, channels)
    key_index = jnp.arange(gathered_rows, dtype=jnp.int32)
    key_shard = key_index // (2 * row_count)
    key_source = (key_index // row_count) % 2
    key_pos = ((row_index - key_source) * half + key_shard) * row_count + key_index % row_count
    visible = (key_pos[None, :] >= seq_start) & (key_pos[None, :] <= query_pos[:, None])

    head_outputs = []
    for head in range(local_heads):
        lanes = slice(head * HEAD_DIM, (head + 1) * HEAD_DIM)
        scores = (
            lax.dot_general(
                query_rows[:, lanes],
                keys_all[:, lanes],
                (((1,), (1,)), ((), ())),
                preferred_element_type=jnp.float32,
            )
            * score_scale
        )
        scores = jnp.where(visible, scores, NEGATIVE)
        row_peak = jnp.max(scores, axis=1, keepdims=True)
        exp_terms = jnp.where(visible, jnp.exp(scores - row_peak), 0.0)
        row_total = jnp.sum(exp_terms, axis=1, keepdims=True)
        weights, row_total = lax.optimization_barrier((exp_terms.astype(jnp.bfloat16), row_total))
        weighted = jnp.dot(weights, values_all[:, lanes], preferred_element_type=jnp.float32)
        head_outputs.append((weighted / row_total).astype(jnp.bfloat16))
    attended = jnp.concatenate(head_outputs, axis=1)
    return (mixed, attended)


def solution(mesh):
    def run(outer_gate, inner_gate, stream, filters, query_rows, key_rows):
        ctx = mesh.shape["ctx"]
        row_count = outer_gate.shape[0] // ctx
        half = (LENGTH // 2) // row_count
        rows = ctx // half
        devices = mesh.devices.reshape(rows, half // CORES, CORES, mesh.shape["tp"])
        split = Mesh(devices, CTX_AXES + ("tp",))
        rows_spec = P(CTX_AXES, "tp")
        in_specs = (rows_spec, rows_spec, rows_spec, P("tp", None), rows_spec, rows_spec)
        outs = jax.shard_map(
            functools.partial(body, rows=rows, half=half),
            mesh=split,
            in_specs=in_specs,
            out_specs=(rows_spec, rows_spec),
            check_vma=False,
        )(outer_gate, inner_gate, stream, filters, query_rows, key_rows)
        placed = NamedSharding(mesh, P("ctx", "tp"))
        return tuple(lax.with_sharding_constraint(o, placed) for o in outs)

    return run
```

```python
import functools
import math

import jax
import jax.numpy as jnp
from jax import lax
from jax.sharding import Mesh, NamedSharding
from jax.sharding import PartitionSpec as P

HEAD_DIM = 128
LENGTH = 8192
CORES = 2
WINDOW_SHARDS = 8

NEGATIVE = -1e30
CTX_AXES = ("row", "col", "core")


def passed_along(block, axis, size, distance):
    route = [(i - distance, i) for i in range(size) if i - distance >= 0]
    return lax.ppermute(block, axis, route)


def toeplitz_taps(filters, offset):
    groups, kernel = filters.shape
    lag = jnp.arange(kernel, dtype=jnp.int32)[:, None, None]
    out_row = jnp.arange(kernel, dtype=jnp.int32)[None, :, None]
    in_row = jnp.arange(kernel, dtype=jnp.int32)[None, None, :]
    picks = (out_row - in_row + offset == lag).astype(filters.dtype).reshape(kernel, kernel * kernel)
    taps = jnp.dot(filters, picks, preferred_element_type=jnp.float32)
    return taps.astype(filters.dtype).reshape(groups, kernel, kernel)


def apply_blocks(matrix, blocks):
    return jnp.einsum("gts,bsgc->btgc", matrix, blocks, preferred_element_type=jnp.float32)


def body(outer_gate, inner_gate, stream, filters, query_rows, key_rows, *, rows, half):
    row_count, channels = outer_gate.shape
    groups, kernel = filters.shape
    group_size = channels // groups
    seq_span = 2 * half
    ctx_size = rows * half
    in_row = lax.axis_index("col") * CORES + lax.axis_index("core")
    row_index = lax.axis_index("row")
    shard_index = row_index * half + in_row
    seq_place = (shard_index + half) % seq_span
    product = (inner_gate.astype(jnp.float32) * stream.astype(jnp.float32)).astype(jnp.bfloat16)
    blocks = product.reshape(row_count // kernel, kernel, groups, group_size)
    near_taps = toeplitz_taps(filters, 0)
    far_taps = toeplitz_taps(filters, kernel)
    tail_rows = product[row_count - kernel + 1 :]
    earlier = passed_along(tail_rows, CTX_AXES, ctx_size, 1)
    earlier = jnp.where(seq_place == 0, jnp.zeros_like(earlier), earlier)
    first_block = jnp.concatenate([jnp.zeros((1, channels), jnp.bfloat16), earlier], 0)
    first_block = first_block.reshape(1, kernel, groups, group_size)
    before = jnp.concatenate([first_block, blocks[:-1]], 0)
    filtered = (apply_blocks(near_taps, blocks) + apply_blocks(far_taps, before)).reshape(
        row_count, channels
    )
    mixed = (outer_gate.astype(jnp.float32) * filtered).astype(jnp.bfloat16)
    local_heads = channels // HEAD_DIM
    queries = query_rows.reshape(row_count, local_heads, HEAD_DIM)
    score_scale = 1.0 / math.sqrt(HEAD_DIM)
    query_pos = shard_index * row_count + jnp.arange(row_count, dtype=jnp.int32)
    seq_start = jnp.maximum(shard_index - seq_place, 0) * row_count

    def row_gather(array):
        gathered = lax.all_gather(array, ("col", "core"), axis=0)
        return gathered.reshape(half * row_count, channels)

    row_up = [(r + 1, r) for r in range(rows - 1)]
    row_down = [(r, r + 1) for r in range(rows - 1)]
    queries_below = lax.ppermute(query_rows, "row", row_up)
    keys_row = row_gather(key_rows)
    values_row = row_gather(mixed)
    key_pos = row_index * half * row_count + jnp.arange(half * row_count, dtype=jnp.int32)
    shard_below = shard_index + half
    place_below = (shard_below + half) % seq_span
    start_below = jnp.maximum(shard_below - place_below, 0) * row_count
    pos_below = shard_below * row_count + jnp.arange(row_count, dtype=jnp.int32)
    visible_own = (key_pos[None, :] >= seq_start) & (key_pos[None, :] <= query_pos[:, None])
    visible_below = (key_pos[None, :] >= start_below) & (key_pos[None, :] <= pos_below[:, None])

    def softmax_part(queries, visible, head):
        lanes = slice(head * HEAD_DIM, (head + 1) * HEAD_DIM)
        scores = (
            lax.dot_general(
                queries[:, lanes],
                keys_row[:, lanes],
                (((1,), (1,)), ((), ())),
                preferred_element_type=jnp.float32,
            )
            * score_scale
        )
        scores = jnp.where(visible, scores, NEGATIVE)
        row_peak = jnp.max(scores, axis=1, keepdims=True)
        exp_terms = jnp.where(visible, jnp.exp(scores - row_peak), 0.0)
        row_total = jnp.sum(exp_terms, axis=1, keepdims=True)
        return lax.optimization_barrier((exp_terms.astype(jnp.bfloat16), row_peak, row_total))

    def weighted_part(weights, head):
        lanes = slice(head * HEAD_DIM, (head + 1) * HEAD_DIM)
        return jnp.dot(weights, values_row[:, lanes], preferred_element_type=jnp.float32)

    below_parts = [softmax_part(queries_below, visible_below, head) for head in range(local_heads)]
    own_parts = [softmax_part(query_rows, visible_own, head) for head in range(local_heads)]
    below_sums = jnp.concatenate(
        [weighted_part(weights, head) for head, (weights, _, _) in enumerate(below_parts)], axis=1
    )
    below_stats = jnp.concatenate(
        [jnp.concatenate([peak, total], axis=1) for _, peak, total in below_parts], axis=1
    )
    above_sums, above_stats = lax.ppermute((below_sums, below_stats), "row", row_down)

    head_outputs = []
    for head, (weights, own_peak, own_total) in enumerate(own_parts):
        own_sum = weighted_part(weights, head)
        lanes = slice(head * HEAD_DIM, (head + 1) * HEAD_DIM)
        above_total = above_stats[:, 2 * head + 1 : 2 * head + 2]
        above_peak = jnp.where(
            above_total > 0, above_stats[:, 2 * head : 2 * head + 1], NEGATIVE
        )
        row_peak = jnp.maximum(own_peak, above_peak)
        own_scale = jnp.exp(own_peak - row_peak)
        above_scale = jnp.exp(above_peak - row_peak)
        total = own_total * own_scale + above_total * above_scale
        weighted = own_sum * own_scale + above_sums[:, lanes] * above_scale
        head_outputs.append((weighted / total).astype(jnp.bfloat16))
    attended = jnp.concatenate(head_outputs, axis=1)
    return (mixed, attended)


def solution(mesh):
    def run(outer_gate, inner_gate, stream, filters, query_rows, key_rows):
        ctx = mesh.shape["ctx"]
        row_count = outer_gate.shape[0] // ctx
        half = (LENGTH // 2) // row_count
        rows = ctx // half
        devices = mesh.devices.reshape(rows, half // CORES, CORES, mesh.shape["tp"])
        split = Mesh(devices, CTX_AXES + ("tp",))
        rows_spec = P(CTX_AXES, "tp")
        in_specs = (rows_spec, rows_spec, rows_spec, P("tp", None), rows_spec, rows_spec)
        outs = jax.shard_map(
            functools.partial(body, rows=rows, half=half),
            mesh=split,
            in_specs=in_specs,
            out_specs=(rows_spec, rows_spec),
            check_vma=False,
        )(outer_gate, inner_gate, stream, filters, query_rows, key_rows)
        placed = NamedSharding(mesh, P("ctx", "tp"))
        return tuple(lax.with_sharding_constraint(o, placed) for o in outs)

    return run
```

```python
import functools
import math

import jax
import jax.numpy as jnp
from jax import lax
from jax.sharding import Mesh, NamedSharding
from jax.sharding import PartitionSpec as P

HEAD_DIM = 128
LENGTH = 8192
CORES = 2
WINDOW_SHARDS = 8

NEGATIVE = -1e30
CTX_AXES = ("row", "col", "core")


def passed_along(block, axis, size, distance):
    route = [(i - distance, i) for i in range(size) if i - distance >= 0]
    return lax.ppermute(block, axis, route)


def toeplitz_taps(filters, offset):
    groups, kernel = filters.shape
    lag = jnp.arange(kernel, dtype=jnp.int32)[:, None, None]
    out_row = jnp.arange(kernel, dtype=jnp.int32)[None, :, None]
    in_row = jnp.arange(kernel, dtype=jnp.int32)[None, None, :]
    picks = (out_row - in_row + offset == lag).astype(filters.dtype).reshape(kernel, kernel * kernel)
    taps = jnp.dot(filters, picks, preferred_element_type=jnp.float32)
    return taps.astype(filters.dtype).reshape(groups, kernel, kernel)


def apply_blocks(matrix, blocks):
    return jnp.einsum("gts,bsgc->btgc", matrix, blocks, preferred_element_type=jnp.float32)


def body(outer_gate, inner_gate, stream, filters, query_rows, key_rows, *, rows, half):
    row_count, channels = outer_gate.shape
    groups, kernel = filters.shape
    group_size = channels // groups
    seq_span = 2 * half
    ctx_size = rows * half
    in_row = lax.axis_index("col") * CORES + lax.axis_index("core")
    row_index = lax.axis_index("row")
    shard_index = row_index * half + in_row
    seq_place = (shard_index + half) % seq_span
    product = (inner_gate.astype(jnp.float32) * stream.astype(jnp.float32)).astype(jnp.bfloat16)
    blocks = product.reshape(row_count // kernel, kernel, groups, group_size)
    near_taps = toeplitz_taps(filters, 0)
    far_taps = toeplitz_taps(filters, kernel)
    tail_rows = product[row_count - kernel + 1 :]
    earlier = passed_along(tail_rows, CTX_AXES, ctx_size, 1)
    earlier = jnp.where(seq_place == 0, jnp.zeros_like(earlier), earlier)
    first_block = jnp.concatenate([jnp.zeros((1, channels), jnp.bfloat16), earlier], 0)
    first_block = first_block.reshape(1, kernel, groups, group_size)
    before = jnp.concatenate([first_block, blocks[:-1]], 0)
    filtered = (apply_blocks(near_taps, blocks) + apply_blocks(far_taps, before)).reshape(
        row_count, channels
    )
    mixed = (outer_gate.astype(jnp.float32) * filtered).astype(jnp.bfloat16)
    local_heads = channels // HEAD_DIM
    queries = query_rows.reshape(row_count, local_heads, HEAD_DIM)
    score_scale = 1.0 / math.sqrt(HEAD_DIM)
    query_pos = shard_index * row_count + jnp.arange(row_count, dtype=jnp.int32)
    seq_start = jnp.maximum(shard_index - seq_place, 0) * row_count

    def row_gather(array):
        gathered = lax.all_gather(array, ("col", "core"), axis=0)
        return gathered.reshape(half * row_count, channels)

    row_up = [(r + 1, r) for r in range(rows - 1)]
    row_down = [(r, r + 1) for r in range(rows - 1)]
    queries_below = lax.ppermute(query_rows, "row", row_up)
    keys_row = row_gather(key_rows)
    values_row = row_gather(mixed)
    key_pos = row_index * half * row_count + jnp.arange(half * row_count, dtype=jnp.int32)
    shard_below = shard_index + half
    place_below = (shard_below + half) % seq_span
    start_below = jnp.maximum(shard_below - place_below, 0) * row_count
    pos_below = shard_below * row_count + jnp.arange(row_count, dtype=jnp.int32)
    visible_own = (key_pos[None, :] >= seq_start) & (key_pos[None, :] <= query_pos[:, None])
    visible_below = (key_pos[None, :] >= start_below) & (key_pos[None, :] <= pos_below[:, None])

    def softmax_part(queries, visible, head):
        lanes = slice(head * HEAD_DIM, (head + 1) * HEAD_DIM)
        scores = (
            lax.dot_general(
                queries[:, lanes],
                keys_row[:, lanes],
                (((1,), (1,)), ((), ())),
                preferred_element_type=jnp.float32,
            )
            * score_scale
        )
        scores = jnp.where(visible, scores, NEGATIVE)
        row_peak = jnp.max(scores, axis=1, keepdims=True)
        exp_terms = jnp.where(visible, jnp.exp(scores - row_peak), 0.0)
        row_total = jnp.sum(exp_terms, axis=1, keepdims=True)
        return lax.optimization_barrier((exp_terms.astype(jnp.bfloat16), row_peak, row_total))

    def weighted_part(weights, head):
        lanes = slice(head * HEAD_DIM, (head + 1) * HEAD_DIM)
        return jnp.dot(weights, values_row[:, lanes], preferred_element_type=jnp.float32)

    below_parts = [softmax_part(queries_below, visible_below, head) for head in range(local_heads)]
    own_parts = [softmax_part(query_rows, visible_own, head) for head in range(local_heads)]
    below_sums = jnp.concatenate(
        [weighted_part(weights, head) for head, (weights, _, _) in enumerate(below_parts)], axis=1
    )
    below_stats = jnp.concatenate(
        [jnp.concatenate([peak, total], axis=1) for _, peak, total in below_parts], axis=1
    )
    below_sums, below_stats, own_weights = lax.optimization_barrier(
        (below_sums, below_stats, [weights for weights, _, _ in own_parts])
    )
    above_sums, above_stats = lax.ppermute((below_sums, below_stats), "row", row_down)

    head_outputs = []
    for head, (weights, (_, own_peak, own_total)) in enumerate(zip(own_weights, own_parts)):
        own_sum = weighted_part(weights, head)
        lanes = slice(head * HEAD_DIM, (head + 1) * HEAD_DIM)
        above_total = above_stats[:, 2 * head + 1 : 2 * head + 2]
        above_peak = jnp.where(
            above_total > 0, above_stats[:, 2 * head : 2 * head + 1], NEGATIVE
        )
        row_peak = jnp.maximum(own_peak, above_peak)
        own_scale = jnp.exp(own_peak - row_peak)
        above_scale = jnp.exp(above_peak - row_peak)
        total = own_total * own_scale + above_total * above_scale
        weighted = own_sum * own_scale + above_sums[:, lanes] * above_scale
        head_outputs.append((weighted / total).astype(jnp.bfloat16))
    attended = jnp.concatenate(head_outputs, axis=1)
    return (mixed, attended)


def solution(mesh):
    def run(outer_gate, inner_gate, stream, filters, query_rows, key_rows):
        ctx = mesh.shape["ctx"]
        row_count = outer_gate.shape[0] // ctx
        half = (LENGTH // 2) // row_count
        rows = ctx // half
        devices = mesh.devices.reshape(rows, half // CORES, CORES, mesh.shape["tp"])
        split = Mesh(devices, CTX_AXES + ("tp",))
        rows_spec = P(CTX_AXES, "tp")
        in_specs = (rows_spec, rows_spec, rows_spec, P("tp", None), rows_spec, rows_spec)
        outs = jax.shard_map(
            functools.partial(body, rows=rows, half=half),
            mesh=split,
            in_specs=in_specs,
            out_specs=(rows_spec, rows_spec),
            check_vma=False,
        )(outer_gate, inner_gate, stream, filters, query_rows, key_rows)
        placed = NamedSharding(mesh, P("ctx", "tp"))
        return tuple(lax.with_sharding_constraint(o, placed) for o in outs)

    return run
```

```python
import functools
import math

import jax
import jax.numpy as jnp
from jax import lax
from jax.sharding import Mesh, NamedSharding
from jax.sharding import PartitionSpec as P

HEAD_DIM = 128
LENGTH = 8192
CORES = 2
WINDOW_SHARDS = 8

NEGATIVE = -1e30
CTX_AXES = ("row", "col", "core")


def passed_along(block, axis, size, distance):
    route = [(i - distance, i) for i in range(size) if i - distance >= 0]
    return lax.ppermute(block, axis, route)


def toeplitz_taps(filters, offset):
    groups, kernel = filters.shape
    lag = jnp.arange(kernel, dtype=jnp.int32)[:, None, None]
    out_row = jnp.arange(kernel, dtype=jnp.int32)[None, :, None]
    in_row = jnp.arange(kernel, dtype=jnp.int32)[None, None, :]
    picks = (out_row - in_row + offset == lag).astype(filters.dtype).reshape(kernel, kernel * kernel)
    taps = jnp.dot(filters, picks, preferred_element_type=jnp.float32)
    return taps.astype(filters.dtype).reshape(groups, kernel, kernel)


def apply_blocks(matrix, blocks):
    return jnp.einsum("gts,bsgc->btgc", matrix, blocks, preferred_element_type=jnp.float32)


def body(outer_gate, inner_gate, stream, filters, query_rows, key_rows, *, rows, half):
    row_count, channels = outer_gate.shape
    groups, kernel = filters.shape
    group_size = channels // groups
    seq_span = 2 * half
    ctx_size = rows * half
    in_row = lax.axis_index("col") * CORES + lax.axis_index("core")
    row_index = lax.axis_index("row")
    shard_index = row_index * half + in_row
    seq_place = (shard_index + half) % seq_span
    product = (inner_gate.astype(jnp.float32) * stream.astype(jnp.float32)).astype(jnp.bfloat16)
    blocks = product.reshape(row_count // kernel, kernel, groups, group_size)
    near_taps = toeplitz_taps(filters, 0)
    far_taps = toeplitz_taps(filters, kernel)
    tail_rows = product[row_count - kernel + 1 :]
    earlier = passed_along(tail_rows, CTX_AXES, ctx_size, 1)
    earlier = jnp.where(seq_place == 0, jnp.zeros_like(earlier), earlier)
    first_block = jnp.concatenate([jnp.zeros((1, channels), jnp.bfloat16), earlier], 0)
    first_block = first_block.reshape(1, kernel, groups, group_size)
    before = jnp.concatenate([first_block, blocks[:-1]], 0)
    filtered = (apply_blocks(near_taps, blocks) + apply_blocks(far_taps, before)).reshape(
        row_count, channels
    )
    mixed = (outer_gate.astype(jnp.float32) * filtered).astype(jnp.bfloat16)
    local_heads = channels // HEAD_DIM
    queries = query_rows.reshape(row_count, local_heads, HEAD_DIM)
    score_scale = 1.0 / math.sqrt(HEAD_DIM)
    query_pos = shard_index * row_count + jnp.arange(row_count, dtype=jnp.int32)
    seq_start = jnp.maximum(shard_index - seq_place, 0) * row_count

    def row_gather(array):
        gathered = lax.all_gather(array, ("col", "core"), axis=0)
        return gathered.reshape(half * row_count, channels)

    row_up = [(r + 1, r) for r in range(rows - 1)]
    row_down = [(r, r + 1) for r in range(rows - 1)]
    queries_below = lax.ppermute(query_rows, "row", row_up)
    keys_row = row_gather(key_rows)
    values_row = row_gather(mixed)
    key_pos = row_index * half * row_count + jnp.arange(half * row_count, dtype=jnp.int32)
    shard_below = shard_index + half
    place_below = (shard_below + half) % seq_span
    start_below = jnp.maximum(shard_below - place_below, 0) * row_count
    pos_below = shard_below * row_count + jnp.arange(row_count, dtype=jnp.int32)
    visible_own = (key_pos[None, :] >= seq_start) & (key_pos[None, :] <= query_pos[:, None])
    visible_below = (key_pos[None, :] >= start_below) & (key_pos[None, :] <= pos_below[:, None])

    def softmax_part(queries, visible, head):
        lanes = slice(head * HEAD_DIM, (head + 1) * HEAD_DIM)
        scores = (
            lax.dot_general(
                queries[:, lanes],
                keys_row[:, lanes],
                (((1,), (1,)), ((), ())),
                preferred_element_type=jnp.float32,
            )
            * score_scale
        )
        scores = jnp.where(visible, scores, NEGATIVE)
        row_peak = jnp.max(scores, axis=1, keepdims=True)
        exp_terms = jnp.where(visible, jnp.exp(scores - row_peak), 0.0)
        row_total = jnp.sum(exp_terms, axis=1, keepdims=True)
        return lax.optimization_barrier((exp_terms.astype(jnp.bfloat16), row_peak, row_total))

    def weighted_part(weights, head):
        lanes = slice(head * HEAD_DIM, (head + 1) * HEAD_DIM)
        return jnp.dot(weights, values_row[:, lanes], preferred_element_type=jnp.float32)

    below_parts = [softmax_part(queries_below, visible_below, head) for head in range(local_heads)]
    own_parts = [softmax_part(query_rows, visible_own, head) for head in range(local_heads)]
    below_sums = jnp.concatenate(
        [weighted_part(weights, head) for head, (weights, _, _) in enumerate(below_parts)], axis=1
    )
    below_stats = jnp.concatenate(
        [jnp.concatenate([peak, total], axis=1) for _, peak, total in below_parts], axis=1
    )
    below_sums, below_stats, own_weights = lax.optimization_barrier(
        (below_sums, below_stats, [weights for weights, _, _ in own_parts])
    )
    stat_lanes = 2 * local_heads
    packed = jnp.concatenate(
        [below_sums, below_stats, jnp.zeros((row_count, HEAD_DIM - stat_lanes), jnp.float32)], axis=1
    )
    packed = lax.ppermute(packed, "row", row_down)
    above_sums = packed[:, :channels]
    above_stats = packed[:, channels : channels + stat_lanes]

    head_outputs = []
    for head, (weights, (_, own_peak, own_total)) in enumerate(zip(own_weights, own_parts)):
        own_sum = weighted_part(weights, head)
        lanes = slice(head * HEAD_DIM, (head + 1) * HEAD_DIM)
        above_total = above_stats[:, 2 * head + 1 : 2 * head + 2]
        above_peak = jnp.where(
            above_total > 0, above_stats[:, 2 * head : 2 * head + 1], NEGATIVE
        )
        row_peak = jnp.maximum(own_peak, above_peak)
        own_scale = jnp.exp(own_peak - row_peak)
        above_scale = jnp.exp(above_peak - row_peak)
        total = own_total * own_scale + above_total * above_scale
        weighted = own_sum * own_scale + above_sums[:, lanes] * above_scale
        head_outputs.append((weighted / total).astype(jnp.bfloat16))
    attended = jnp.concatenate(head_outputs, axis=1)
    return (mixed, attended)


def solution(mesh):
    def run(outer_gate, inner_gate, stream, filters, query_rows, key_rows):
        ctx = mesh.shape["ctx"]
        row_count = outer_gate.shape[0] // ctx
        half = (LENGTH // 2) // row_count
        rows = ctx // half
        devices = mesh.devices.reshape(rows, half // CORES, CORES, mesh.shape["tp"])
        split = Mesh(devices, CTX_AXES + ("tp",))
        rows_spec = P(CTX_AXES, "tp")
        in_specs = (rows_spec, rows_spec, rows_spec, P("tp", None), rows_spec, rows_spec)
        outs = jax.shard_map(
            functools.partial(body, rows=rows, half=half),
            mesh=split,
            in_specs=in_specs,
            out_specs=(rows_spec, rows_spec),
            check_vma=False,
        )(outer_gate, inner_gate, stream, filters, query_rows, key_rows)
        placed = NamedSharding(mesh, P("ctx", "tp"))
        return tuple(lax.with_sharding_constraint(o, placed) for o in outs)

    return run
```

```python
import functools
import math

import jax
import jax.numpy as jnp
from jax import lax
from jax.sharding import Mesh, NamedSharding
from jax.sharding import PartitionSpec as P

HEAD_DIM = 128
LENGTH = 8192
CORES = 2
WINDOW_SHARDS = 8

NEGATIVE = -1e30
CTX_AXES = ("row", "col", "core")


def passed_along(block, axis, size, distance):
    route = [(i - distance, i) for i in range(size) if i - distance >= 0]
    return lax.ppermute(block, axis, route)


def toeplitz_taps(filters, offset):
    groups, kernel = filters.shape
    lag = jnp.arange(kernel, dtype=jnp.int32)[:, None, None]
    out_row = jnp.arange(kernel, dtype=jnp.int32)[None, :, None]
    in_row = jnp.arange(kernel, dtype=jnp.int32)[None, None, :]
    picks = (out_row - in_row + offset == lag).astype(filters.dtype).reshape(kernel, kernel * kernel)
    taps = jnp.dot(filters, picks, preferred_element_type=jnp.float32)
    return taps.astype(filters.dtype).reshape(groups, kernel, kernel)


def apply_blocks(matrix, blocks):
    return jnp.einsum("gts,bsgc->btgc", matrix, blocks, preferred_element_type=jnp.float32)


def body(outer_gate, inner_gate, stream, filters, query_rows, key_rows, *, rows, half):
    row_count, channels = outer_gate.shape
    groups, kernel = filters.shape
    group_size = channels // groups
    seq_span = 2 * half
    ctx_size = rows * half
    in_row = lax.axis_index("col") * CORES + lax.axis_index("core")
    row_index = lax.axis_index("row")
    shard_index = row_index * half + in_row
    seq_place = (shard_index + half) % seq_span
    product = (inner_gate.astype(jnp.float32) * stream.astype(jnp.float32)).astype(jnp.bfloat16)
    blocks = product.reshape(row_count // kernel, kernel, groups, group_size)
    near_taps = toeplitz_taps(filters, 0)
    far_taps = toeplitz_taps(filters, kernel)
    tail_rows = product[row_count - kernel + 1 :]
    earlier = passed_along(tail_rows, CTX_AXES, ctx_size, 1)
    earlier = jnp.where(seq_place == 0, jnp.zeros_like(earlier), earlier)
    first_block = jnp.concatenate([jnp.zeros((1, channels), jnp.bfloat16), earlier], 0)
    first_block = first_block.reshape(1, kernel, groups, group_size)
    before = jnp.concatenate([first_block, blocks[:-1]], 0)
    filtered = (apply_blocks(near_taps, blocks) + apply_blocks(far_taps, before)).reshape(
        row_count, channels
    )
    mixed = (outer_gate.astype(jnp.float32) * filtered).astype(jnp.bfloat16)
    local_heads = channels // HEAD_DIM
    queries = query_rows.reshape(row_count, local_heads, HEAD_DIM)
    score_scale = 1.0 / math.sqrt(HEAD_DIM)
    query_pos = shard_index * row_count + jnp.arange(row_count, dtype=jnp.int32)
    seq_start = jnp.maximum(shard_index - seq_place, 0) * row_count

    def row_gather(array):
        gathered = lax.all_gather(array, ("col", "core"), axis=0)
        return gathered.reshape(half * row_count, channels)

    row_up = [(r + 1, r) for r in range(rows - 1)]
    row_down = [(r, r + 1) for r in range(rows - 1)]
    queries_below = lax.ppermute(query_rows, "row", row_up)
    keys_row = row_gather(key_rows)
    values_row = row_gather(mixed)
    key_pos = row_index * half * row_count + jnp.arange(half * row_count, dtype=jnp.int32)
    shard_below = shard_index + half
    place_below = (shard_below + half) % seq_span
    start_below = jnp.maximum(shard_below - place_below, 0) * row_count
    pos_below = shard_below * row_count + jnp.arange(row_count, dtype=jnp.int32)
    visible_own = (key_pos[None, :] >= seq_start) & (key_pos[None, :] <= query_pos[:, None])
    visible_below = (key_pos[None, :] >= start_below) & (key_pos[None, :] <= pos_below[:, None])

    def softmax_part(queries, visible, head):
        lanes = slice(head * HEAD_DIM, (head + 1) * HEAD_DIM)
        scores = (
            lax.dot_general(
                queries[:, lanes],
                keys_row[:, lanes],
                (((1,), (1,)), ((), ())),
                preferred_element_type=jnp.float32,
            )
            * score_scale
        )
        scores = jnp.where(visible, scores, NEGATIVE)
        row_peak = jnp.max(scores, axis=1, keepdims=True)
        exp_terms = jnp.where(visible, jnp.exp(scores - row_peak), 0.0)
        row_total = jnp.sum(exp_terms, axis=1, keepdims=True)
        return lax.optimization_barrier((exp_terms.astype(jnp.bfloat16), row_peak, row_total))

    def weighted_part(weights, head):
        lanes = slice(head * HEAD_DIM, (head + 1) * HEAD_DIM)
        return jnp.dot(weights, values_row[:, lanes], preferred_element_type=jnp.float32)

    below_parts = [softmax_part(queries_below, visible_below, head) for head in range(local_heads)]
    own_parts = [softmax_part(query_rows, visible_own, head) for head in range(local_heads)]
    below_sums = jnp.concatenate(
        [weighted_part(weights, head) for head, (weights, _, _) in enumerate(below_parts)], axis=1
    )
    below_stats = jnp.concatenate(
        [jnp.concatenate([peak, total], axis=1) for _, peak, total in below_parts], axis=1
    )
    below_sums, below_stats, own_weights = lax.optimization_barrier(
        (below_sums, below_stats, [weights for weights, _, _ in own_parts])
    )
    above_sums, above_stats = lax.ppermute(
        (below_sums.astype(jnp.bfloat16), below_stats), "row", row_down
    )
    above_sums = above_sums.astype(jnp.float32)

    head_outputs = []
    for head, (weights, (_, own_peak, own_total)) in enumerate(zip(own_weights, own_parts)):
        own_sum = weighted_part(weights, head)
        lanes = slice(head * HEAD_DIM, (head + 1) * HEAD_DIM)
        above_total = above_stats[:, 2 * head + 1 : 2 * head + 2]
        above_peak = jnp.where(
            above_total > 0, above_stats[:, 2 * head : 2 * head + 1], NEGATIVE
        )
        row_peak = jnp.maximum(own_peak, above_peak)
        own_scale = jnp.exp(own_peak - row_peak)
        above_scale = jnp.exp(above_peak - row_peak)
        total = own_total * own_scale + above_total * above_scale
        weighted = own_sum * own_scale + above_sums[:, lanes] * above_scale
        head_outputs.append((weighted / total).astype(jnp.bfloat16))
    attended = jnp.concatenate(head_outputs, axis=1)
    return (mixed, attended)


def solution(mesh):
    def run(outer_gate, inner_gate, stream, filters, query_rows, key_rows):
        ctx = mesh.shape["ctx"]
        row_count = outer_gate.shape[0] // ctx
        half = (LENGTH // 2) // row_count
        rows = ctx // half
        devices = mesh.devices.reshape(rows, half // CORES, CORES, mesh.shape["tp"])
        split = Mesh(devices, CTX_AXES + ("tp",))
        rows_spec = P(CTX_AXES, "tp")
        in_specs = (rows_spec, rows_spec, rows_spec, P("tp", None), rows_spec, rows_spec)
        outs = jax.shard_map(
            functools.partial(body, rows=rows, half=half),
            mesh=split,
            in_specs=in_specs,
            out_specs=(rows_spec, rows_spec),
            check_vma=False,
        )(outer_gate, inner_gate, stream, filters, query_rows, key_rows)
        placed = NamedSharding(mesh, P("ctx", "tp"))
        return tuple(lax.with_sharding_constraint(o, placed) for o in outs)

    return run
```

```python
import functools
import math

import jax
import jax.numpy as jnp
from jax import lax
from jax.sharding import Mesh, NamedSharding
from jax.sharding import PartitionSpec as P

HEAD_DIM = 128
LENGTH = 8192
CORES = 2
WINDOW_SHARDS = 8

NEGATIVE = -1e30
CTX_AXES = ("row", "col", "core")


def passed_along(block, axis, size, distance):
    route = [(i - distance, i) for i in range(size) if i - distance >= 0]
    return lax.ppermute(block, axis, route)


def toeplitz_taps(filters, offset):
    groups, kernel = filters.shape
    lag = jnp.arange(kernel, dtype=jnp.int32)[:, None, None]
    out_row = jnp.arange(kernel, dtype=jnp.int32)[None, :, None]
    in_row = jnp.arange(kernel, dtype=jnp.int32)[None, None, :]
    picks = (out_row - in_row + offset == lag).astype(filters.dtype).reshape(kernel, kernel * kernel)
    taps = jnp.dot(filters, picks, preferred_element_type=jnp.float32)
    return taps.astype(filters.dtype).reshape(groups, kernel, kernel)


def apply_blocks(matrix, blocks):
    return jnp.einsum("gts,bsgc->btgc", matrix, blocks, preferred_element_type=jnp.float32)


def body(outer_gate, inner_gate, stream, filters, query_rows, key_rows, *, rows, half):
    row_count, channels = outer_gate.shape
    groups, kernel = filters.shape
    group_size = channels // groups
    seq_span = 2 * half
    ctx_size = rows * half
    in_row = lax.axis_index("col") * CORES + lax.axis_index("core")
    row_index = lax.axis_index("row")
    shard_index = row_index * half + in_row
    seq_place = (shard_index + half) % seq_span
    product = (inner_gate.astype(jnp.float32) * stream.astype(jnp.float32)).astype(jnp.bfloat16)
    blocks = product.reshape(row_count // kernel, kernel, groups, group_size)
    near_taps = toeplitz_taps(filters, 0)
    far_taps = toeplitz_taps(filters, kernel)
    tail_rows = product[row_count - kernel + 1 :]
    earlier = passed_along(tail_rows, CTX_AXES, ctx_size, 1)
    earlier = jnp.where(seq_place == 0, jnp.zeros_like(earlier), earlier)
    first_block = jnp.concatenate([jnp.zeros((1, channels), jnp.bfloat16), earlier], 0)
    first_block = first_block.reshape(1, kernel, groups, group_size)
    before = jnp.concatenate([first_block, blocks[:-1]], 0)
    filtered = (apply_blocks(near_taps, blocks) + apply_blocks(far_taps, before)).reshape(
        row_count, channels
    )
    mixed = (outer_gate.astype(jnp.float32) * filtered).astype(jnp.bfloat16)
    local_heads = channels // HEAD_DIM
    queries = query_rows.reshape(row_count, local_heads, HEAD_DIM)
    score_scale = 1.0 / math.sqrt(HEAD_DIM)
    query_pos = shard_index * row_count + jnp.arange(row_count, dtype=jnp.int32)
    seq_start = jnp.maximum(shard_index - seq_place, 0) * row_count

    def row_gather(array):
        gathered = lax.all_gather(array, ("col", "core"), axis=0)
        return gathered.reshape(half * row_count, channels)

    row_up = [(r + 1, r) for r in range(rows - 1)]
    row_down = [(r, r + 1) for r in range(rows - 1)]
    queries_below = lax.ppermute(query_rows, "row", row_up)
    keys_row = row_gather(key_rows)
    values_row = row_gather(mixed)
    key_pos = row_index * half * row_count + jnp.arange(half * row_count, dtype=jnp.int32)
    shard_below = shard_index + half
    place_below = (shard_below + half) % seq_span
    start_below = jnp.maximum(shard_below - place_below, 0) * row_count
    pos_below = shard_below * row_count + jnp.arange(row_count, dtype=jnp.int32)
    visible_own = (key_pos[None, :] >= seq_start) & (key_pos[None, :] <= query_pos[:, None])
    visible_below = (key_pos[None, :] >= start_below) & (key_pos[None, :] <= pos_below[:, None])

    def softmax_part(queries, visible, head):
        lanes = slice(head * HEAD_DIM, (head + 1) * HEAD_DIM)
        scores = (
            lax.dot_general(
                queries[:, lanes],
                keys_row[:, lanes],
                (((1,), (1,)), ((), ())),
                preferred_element_type=jnp.float32,
            )
            * score_scale
        )
        scores = jnp.where(visible, scores, NEGATIVE)
        row_peak = jnp.max(scores, axis=1, keepdims=True)
        exp_terms = jnp.where(visible, jnp.exp(scores - row_peak), 0.0)
        row_total = jnp.sum(exp_terms, axis=1, keepdims=True)
        return lax.optimization_barrier((exp_terms.astype(jnp.bfloat16), row_peak, row_total))

    def weighted_part(weights, head):
        lanes = slice(head * HEAD_DIM, (head + 1) * HEAD_DIM)
        return jnp.dot(weights, values_row[:, lanes], preferred_element_type=jnp.float32)

    below_parts = [softmax_part(queries_below, visible_below, head) for head in range(local_heads)]
    above_stats = lax.ppermute(
        jnp.concatenate(
            [jnp.concatenate([peak, total], axis=1) for _, peak, total in below_parts], axis=1
        ),
        "row",
        row_down,
    )
    own_parts = [softmax_part(query_rows, visible_own, head) for head in range(local_heads)]
    values_row, above_stats = lax.optimization_barrier((values_row, above_stats))
    below_sums = jnp.concatenate(
        [weighted_part(weights, head) for head, (weights, _, _) in enumerate(below_parts)], axis=1
    )
    below_sums, own_weights = lax.optimization_barrier(
        (below_sums, [weights for weights, _, _ in own_parts])
    )
    above_sums = lax.ppermute(below_sums.astype(jnp.bfloat16), "row", row_down)
    above_sums = above_sums.astype(jnp.float32)

    head_outputs = []
    for head, (weights, (_, own_peak, own_total)) in enumerate(zip(own_weights, own_parts)):
        own_sum = weighted_part(weights, head)
        lanes = slice(head * HEAD_DIM, (head + 1) * HEAD_DIM)
        above_total = above_stats[:, 2 * head + 1 : 2 * head + 2]
        above_peak = jnp.where(
            above_total > 0, above_stats[:, 2 * head : 2 * head + 1], NEGATIVE
        )
        row_peak = jnp.maximum(own_peak, above_peak)
        own_scale = jnp.exp(own_peak - row_peak)
        above_scale = jnp.exp(above_peak - row_peak)
        total = own_total * own_scale + above_total * above_scale
        weighted = own_sum * own_scale + above_sums[:, lanes] * above_scale
        head_outputs.append((weighted / total).astype(jnp.bfloat16))
    attended = jnp.concatenate(head_outputs, axis=1)
    return (mixed, attended)


def solution(mesh):
    def run(outer_gate, inner_gate, stream, filters, query_rows, key_rows):
        ctx = mesh.shape["ctx"]
        row_count = outer_gate.shape[0] // ctx
        half = (LENGTH // 2) // row_count
        rows = ctx // half
        devices = mesh.devices.reshape(rows, half // CORES, CORES, mesh.shape["tp"])
        split = Mesh(devices, CTX_AXES + ("tp",))
        rows_spec = P(CTX_AXES, "tp")
        in_specs = (rows_spec, rows_spec, rows_spec, P("tp", None), rows_spec, rows_spec)
        outs = jax.shard_map(
            functools.partial(body, rows=rows, half=half),
            mesh=split,
            in_specs=in_specs,
            out_specs=(rows_spec, rows_spec),
            check_vma=False,
        )(outer_gate, inner_gate, stream, filters, query_rows, key_rows)
        placed = NamedSharding(mesh, P("ctx", "tp"))
        return tuple(lax.with_sharding_constraint(o, placed) for o in outs)

    return run
```

```python
import functools
import math

import jax
import jax.numpy as jnp
from jax import lax
from jax.sharding import Mesh, NamedSharding
from jax.sharding import PartitionSpec as P

HEAD_DIM = 128
LENGTH = 8192
CORES = 2
WINDOW_SHARDS = 8

NEGATIVE = -1e30
CTX_AXES = ("row", "col", "core")


def passed_along(block, axis, size, distance):
    route = [(i - distance, i) for i in range(size) if i - distance >= 0]
    return lax.ppermute(block, axis, route)


def toeplitz_taps(filters, offset):
    groups, kernel = filters.shape
    lag = jnp.arange(kernel, dtype=jnp.int32)[:, None, None]
    out_row = jnp.arange(kernel, dtype=jnp.int32)[None, :, None]
    in_row = jnp.arange(kernel, dtype=jnp.int32)[None, None, :]
    picks = (out_row - in_row + offset == lag).astype(filters.dtype).reshape(kernel, kernel * kernel)
    taps = jnp.dot(filters, picks, preferred_element_type=jnp.float32)
    return taps.astype(filters.dtype).reshape(groups, kernel, kernel)


def apply_blocks(matrix, blocks):
    return jnp.einsum("gts,bsgc->btgc", matrix, blocks, preferred_element_type=jnp.float32)


def body(outer_gate, inner_gate, stream, filters, query_rows, key_rows, *, rows, half):
    row_count, channels = outer_gate.shape
    groups, kernel = filters.shape
    group_size = channels // groups
    seq_span = 2 * half
    ctx_size = rows * half
    in_row = lax.axis_index("col") * CORES + lax.axis_index("core")
    row_index = lax.axis_index("row")
    shard_index = row_index * half + in_row
    seq_place = (shard_index + half) % seq_span
    product = (inner_gate.astype(jnp.float32) * stream.astype(jnp.float32)).astype(jnp.bfloat16)
    blocks = product.reshape(row_count // kernel, kernel, groups, group_size)
    near_taps = toeplitz_taps(filters, 0)
    far_taps = toeplitz_taps(filters, kernel)
    tail_rows = product[row_count - kernel + 1 :]
    earlier = passed_along(tail_rows, CTX_AXES, ctx_size, 1)
    earlier = jnp.where(seq_place == 0, jnp.zeros_like(earlier), earlier)
    first_block = jnp.concatenate([jnp.zeros((1, channels), jnp.bfloat16), earlier], 0)
    first_block = first_block.reshape(1, kernel, groups, group_size)
    before = jnp.concatenate([first_block, blocks[:-1]], 0)
    filtered = (apply_blocks(near_taps, blocks) + apply_blocks(far_taps, before)).reshape(
        row_count, channels
    )
    mixed = (outer_gate.astype(jnp.float32) * filtered).astype(jnp.bfloat16)
    local_heads = channels // HEAD_DIM
    queries = query_rows.reshape(row_count, local_heads, HEAD_DIM)
    score_scale = 1.0 / math.sqrt(HEAD_DIM)
    query_pos = shard_index * row_count + jnp.arange(row_count, dtype=jnp.int32)
    seq_start = jnp.maximum(shard_index - seq_place, 0) * row_count

    def row_gather(array):
        gathered = lax.all_gather(array, ("col", "core"), axis=0)
        return gathered.reshape(half * row_count, channels)

    row_up = [(r + 1, r) for r in range(rows - 1)]
    row_down = [(r, r + 1) for r in range(rows - 1)]
    queries_below = lax.ppermute(query_rows, "row", row_up)
    keys_row = row_gather(key_rows)
    values_row = row_gather(mixed)
    key_pos = row_index * half * row_count + jnp.arange(half * row_count, dtype=jnp.int32)
    shard_below = shard_index + half
    place_below = (shard_below + half) % seq_span
    start_below = jnp.maximum(shard_below - place_below, 0) * row_count
    pos_below = shard_below * row_count + jnp.arange(row_count, dtype=jnp.int32)
    visible_own = (key_pos[None, :] >= seq_start) & (key_pos[None, :] <= query_pos[:, None])
    visible_below = (key_pos[None, :] >= start_below) & (key_pos[None, :] <= pos_below[:, None])

    def softmax_part(queries, visible, head):
        lanes = slice(head * HEAD_DIM, (head + 1) * HEAD_DIM)
        scores = (
            lax.dot_general(
                queries[:, lanes],
                keys_row[:, lanes],
                (((1,), (1,)), ((), ())),
                preferred_element_type=jnp.float32,
            )
            * score_scale
        )
        scores = jnp.where(visible, scores, NEGATIVE)
        row_peak = jnp.max(scores, axis=1, keepdims=True)
        exp_terms = jnp.where(visible, jnp.exp(scores - row_peak), 0.0)
        row_total = jnp.sum(exp_terms, axis=1, keepdims=True)
        return lax.optimization_barrier((exp_terms.astype(jnp.bfloat16), row_peak, row_total))

    def weighted_part(weights, head):
        lanes = slice(head * HEAD_DIM, (head + 1) * HEAD_DIM)
        return jnp.dot(weights, values_row[:, lanes], preferred_element_type=jnp.float32)

    below_parts = [softmax_part(queries_below, visible_below, head) for head in range(local_heads)]
    above_stats = lax.ppermute(
        jnp.concatenate(
            [jnp.concatenate([peak, total], axis=1) for _, peak, total in below_parts], axis=1
        ),
        "row",
        row_down,
    )
    own_parts = [softmax_part(query_rows, visible_own, head) for head in range(local_heads)]
    values_row, above_stats = lax.optimization_barrier((values_row, above_stats))
    below_sums = jnp.concatenate(
        [weighted_part(weights, head) for head, (weights, _, _) in enumerate(below_parts)], axis=1
    )
    below_sums, own_weights = lax.optimization_barrier(
        (below_sums, [weights for weights, _, _ in own_parts])
    )
    above_sums = lax.ppermute(below_sums.astype(jnp.bfloat16), "row", row_down)
    above_sums = above_sums.astype(jnp.float32)

    own_sums = [weighted_part(weights, head) for head, weights in enumerate(own_weights)]
    above_sums, own_sums = lax.optimization_barrier((above_sums, own_sums))
    head_outputs = []
    for head, (own_sum, (_, own_peak, own_total)) in enumerate(zip(own_sums, own_parts)):
        lanes = slice(head * HEAD_DIM, (head + 1) * HEAD_DIM)
        above_total = above_stats[:, 2 * head + 1 : 2 * head + 2]
        above_peak = jnp.where(
            above_total > 0, above_stats[:, 2 * head : 2 * head + 1], NEGATIVE
        )
        row_peak = jnp.maximum(own_peak, above_peak)
        own_scale = jnp.exp(own_peak - row_peak)
        above_scale = jnp.exp(above_peak - row_peak)
        total = own_total * own_scale + above_total * above_scale
        weighted = own_sum * own_scale + above_sums[:, lanes] * above_scale
        head_outputs.append((weighted / total).astype(jnp.bfloat16))
    attended = jnp.concatenate(head_outputs, axis=1)
    return (mixed, attended)


def solution(mesh):
    def run(outer_gate, inner_gate, stream, filters, query_rows, key_rows):
        ctx = mesh.shape["ctx"]
        row_count = outer_gate.shape[0] // ctx
        half = (LENGTH // 2) // row_count
        rows = ctx // half
        devices = mesh.devices.reshape(rows, half // CORES, CORES, mesh.shape["tp"])
        split = Mesh(devices, CTX_AXES + ("tp",))
        rows_spec = P(CTX_AXES, "tp")
        in_specs = (rows_spec, rows_spec, rows_spec, P("tp", None), rows_spec, rows_spec)
        outs = jax.shard_map(
            functools.partial(body, rows=rows, half=half),
            mesh=split,
            in_specs=in_specs,
            out_specs=(rows_spec, rows_spec),
            check_vma=False,
        )(outer_gate, inner_gate, stream, filters, query_rows, key_rows)
        placed = NamedSharding(mesh, P("ctx", "tp"))
        return tuple(lax.with_sharding_constraint(o, placed) for o in outs)

    return run
```
